1024 devices in a mesh: dp: 64 (over z_lo, y, core), context: 16 (over z_hi, x).
Axes of the slice: x: 8, y: 8, z: 8 (z_hi: 2, z_lo: 4; z = z_hi * 4 + z_lo), core: 2. Of those that a mesh axis runs over, the one named last changes fastest.
Arguments:
- hidden_in: bfloat16 [64, 2048, 2048], P('dp', 'context'), may hold values from -6 to 6
- queries: bfloat16 [64, 2048, 2048], P('dp', 'context'), may hold values from -310 to 310
- kv_weight: bfloat16 [2048, 1024], P('dp'), may hold values from -0.125 to 0.125
- doc_ids: int32 [64, 2048], P('dp'), may hold values from 0 to 7, never falling along the last dimension, each value on 1 to 1152 neighbouring positions
Outputs:
- attn_out: bfloat16 [64, 2048, 2048], P('dp', 'context')
The draws below stay inside these ranges and needn't reach their ends.
Inputs may be any that keep to these rules, and one draw needn't show every extreme that they name: `doc_ids`: document numbers never fall along a sequence; each document holds 1 to 1152 tokens and some document of every sequence holds exactly 1152.
All inputs are finite; a program needn't handle non-finite values.
Results may differ from the reference program's by a relative error of at most 0.028.
Values may be sent and summed in bfloat16 or wider, within the bound.
No kernel may reach another device: no remote copies, remote signals or barrier semaphores. Data moves between devices by JAX's collectives and lax.ppermute only.
A program may use at most 64 MiB of HBM per device.

```python
import math
import jax
import jax.numpy as jnp
import numpy as np
from jax import lax

D = 2048
QUERY_HEADS = 16
KEY_VALUE_HEADS = 4
HEAD_SIZE = 128
SEQUENCE_LENGTH = 2048
SEQS = 64
KVW = 1024
DOC_MOST = 1152
N_CONTEXT = 16


def draw_queries(key, part):
    shape = (SEQS, SEQUENCE_LENGTH, QUERY_HEADS * HEAD_SIZE)
    return jnp.clip(jax.random.normal(key, shape, jnp.float32), -6.0, 6.0).astype(jnp.bfloat16)


def block_scale(rng, shape, shards, smallest, high):
    def one(dim, parts):
        heights = jax.random.uniform(jax.random.fold_in(jax.random.fold_in(rng, 6), dim), (parts,), jnp.float32, smallest / len(shards), high / len(shards))
        return jnp.repeat(jnp.exp(heights), shape[dim] // parts).reshape((-1,) + (1,) * (len(shape) - dim - 1))

    level = one(*shards[0])
    for cut in shards[1:]:
        level = level * one(*cut)
    return level


def split_up(number_of, total, bound, slope):
    loads = [(1 << 20) // math.isqrt(rank ** slope) + 1 for rank in range(2, number_of + 1)]
    surplus, counts = total - bound - (number_of - 1), [1] * (number_of - 1)
    while surplus > 0:
        free = [i for i in range(number_of - 1) if counts[i] < bound]
        mass, budget = sum([loads[i] for i in free]), surplus
        for i in free:
            extra = min(bound - counts[i], max(1, budget * loads[i] // mass), surplus)
            counts[i] = counts[i] + extra
            surplus = surplus - extra
    return np.array([bound] + counts)


def uneven(stream_key, number_of, total, most, skew):
    if number_of == 2:
        one = jax.random.randint(stream_key, (), max(1, total - most), min(most, total - 1) + 1)
        return jnp.stack([one, total - one])
    sizes = jnp.asarray(split_up(number_of, total, most, skew), jnp.int32)
    couples = (number_of - 1) // 2
    donor, sink = sizes[1:1 + 2 * couples:2], sizes[2:2 + 2 * couples:2]
    room = jnp.minimum(donor - 1, most - sink)
    moved = jax.random.randint(jax.random.fold_in(stream_key, 1), (couples,), 0, 1 << 20) % (room + 1)
    sizes = sizes.at[1:1 + 2 * couples:2].set(donor - moved).at[2:2 + 2 * couples:2].set(sink + moved)
    return sizes[jax.random.permutation(jax.random.fold_in(stream_key, 2), number_of)]


def gaussian(key, dims, spread, limit, shards=(), kind=jnp.bfloat16):
    values = jax.random.normal(key, dims, jnp.float32) * spread
    if len(shards) > 0:
        values = block_scale(key, dims, shards, -0.22, 0.18) * values
    return jnp.clip(values, min=-limit, max=limit).astype(kind)


def setup_inputs(seed: int = 0) -> dict:
    arg_keys = jax.random.split(jax.random.key(seed), 5)
    hidden_in = gaussian(arg_keys[0], (SEQS, SEQUENCE_LENGTH, D), 1.0, 6.0, ((0, 64), (1, 16)))
    queries = draw_queries(jax.random.fold_in(arg_keys[4], 71), 0)
    kv_weight = gaussian(arg_keys[2], (D, KVW), D ** -0.5, 0.125, ((0, 64),))
    doc_ids = jax.vmap(lambda own: jnp.searchsorted(jnp.cumsum(uneven(own, N_CONTEXT // 2, SEQUENCE_LENGTH, DOC_MOST, 0)), jnp.arange(SEQUENCE_LENGTH), side="right"))(jax.random.split(arg_keys[3], SEQS)).reshape((SEQS, SEQUENCE_LENGTH)).astype(jnp.int32)
    return {"hidden_in": hidden_in, "queries": queries, "kv_weight": kv_weight, "doc_ids": doc_ids}


NEG = -1.0e30


def apply_rotation(key_rows, positions):
    half = key_rows.shape[-1] // 2
    freq = 500000.0 ** (-(jnp.arange(half, dtype=jnp.float32) * 2.0 / key_rows.shape[-1]))
    angle = positions.astype(jnp.float32)[:, None] * freq[None, :]
    cosine = jnp.cos(angle)[:, None, :]
    sine = jnp.sin(angle)[:, None, :]
    first = key_rows[..., :half]
    second = key_rows[..., half:]
    return jnp.concatenate([first * cosine - second * sine, second * cosine + first * sine], axis=-1)


def reference(hidden_in, queries, kv_weight, doc_ids):
    scale = 1.0 / float(HEAD_SIZE) ** 0.5
    block = min(512, SEQUENCE_LENGTH)
    nblocks = SEQUENCE_LENGTH // block

    def one_sequence(items):
        acts, query_rows_all, ids = items
        key_value = jnp.dot(acts, kv_weight, preferred_element_type=jnp.float32)
        key_positions = jnp.arange(SEQUENCE_LENGTH, dtype=jnp.int32)
        key_rows = apply_rotation(key_value[:, :KEY_VALUE_HEADS * HEAD_SIZE].reshape(SEQUENCE_LENGTH, KEY_VALUE_HEADS, HEAD_SIZE), key_positions).astype(jnp.bfloat16)
        value_rows = key_value[:, KEY_VALUE_HEADS * HEAD_SIZE:].reshape(SEQUENCE_LENGTH, KEY_VALUE_HEADS, HEAD_SIZE).astype(jnp.bfloat16)
        grouped_queries = query_rows_all.reshape(SEQUENCE_LENGTH, KEY_VALUE_HEADS, QUERY_HEADS // KEY_VALUE_HEADS, HEAD_SIZE)
        keys_wide = key_rows.astype(jnp.float32)
        values_wide = value_rows.astype(jnp.float32)

        def one_block(index):
            start = (index * block).astype(jnp.int32)
            query_block = lax.dynamic_slice_in_dim(grouped_queries, start, block, 0).astype(jnp.float32)
            query_pos = start + jnp.arange(block, dtype=jnp.int32)
            query_doc = lax.dynamic_slice_in_dim(ids, start, block, 0)
            allowed = (key_positions[None, :] <= query_pos[:, None]) & (ids[None, :] == query_doc[:, None])
            scores = jnp.einsum("qhgd,khd->hgqk", query_block, keys_wide) * scale
            scores = jnp.where(allowed[None, None], scores, NEG)
            row_max = jnp.max(scores, axis=-1)
            weights = jnp.where(allowed[None, None], jnp.exp(scores - row_max[..., None]), 0.0)
            total = jnp.sum(weights, axis=-1)
            rounded = weights.astype(jnp.bfloat16).astype(jnp.float32)
            sums = jnp.einsum("hgqk,khd->hgqd", rounded, values_wide)
            result = sums / total[..., None]
            return jnp.transpose(result, (2, 0, 1, 3)).reshape(block, QUERY_HEADS * HEAD_SIZE).astype(jnp.bfloat16)

        outs = lax.map(one_block, jnp.arange(nblocks, dtype=jnp.int32))
        return outs.reshape(SEQUENCE_LENGTH, QUERY_HEADS * HEAD_SIZE)

    return lax.map(one_sequence, (hidden_in, queries, doc_ids))
```

```python
import functools

import jax
import jax.numpy as jnp
from jax import lax
from jax.sharding import PartitionSpec as P

HEAD_SIZE = 128
DOC_MOST = 1152

NEG = -1e30


def apply_rotation(key_rows, positions):
    half = key_rows.shape[-1] // 2
    freq = 500000.0 ** (-(jnp.arange(half, dtype=jnp.float32) * 2.0 / key_rows.shape[-1]))
    angle = positions.astype(jnp.float32)[:, None] * freq[None, :]
    cosine = jnp.cos(angle)[:, None, :]
    sine = jnp.sin(angle)[:, None, :]
    first = key_rows[..., :half]
    second = key_rows[..., half:]
    return jnp.concatenate(
        [first * cosine - second * sine, second * cosine + first * sine], axis=-1
    )


def gather_rows(block, axis_name, count):
    index = lax.axis_index(axis_name)
    buf = block[None]
    bits = count.bit_length() - 1
    for b in reversed(range(bits)):
        m = 1 << b
        other = lax.ppermute(buf, axis_name, [(j, j ^ m) for j in range(count)])
        low_side = ((index >> b) & 1) == 0
        lo = jnp.where(low_side, buf, other)
        hi = jnp.where(low_side, other, buf)
        buf = jnp.concatenate([lo[:, None], hi[:, None]], axis=1).reshape((-1,) + block.shape)
    return buf.reshape((-1,) + block.shape[1:])


def shards(n_dp, n_ctx, hidden_in, queries, kv_weight, doc_ids):
    acts = hidden_in[0]
    tok = acts.shape[0]
    columns = kv_weight.shape[1]
    heads_kv = columns // (2 * HEAD_SIZE)
    heads_q = queries.shape[2] // HEAD_SIZE
    group = heads_q // heads_kv
    scale = 1.0 / float(HEAD_SIZE) ** 0.5
    position = lax.axis_index("context")
    weight = gather_rows(kv_weight, "dp", n_dp)
    key_value = jnp.dot(acts, weight, preferred_element_type=jnp.float32)
    query_pos = position * tok + jnp.arange(tok, dtype=jnp.int32)
    key_rows = apply_rotation(
        key_value[:, : heads_kv * HEAD_SIZE].reshape(tok, heads_kv, HEAD_SIZE), query_pos
    ).astype(jnp.bfloat16)
    value_rows = (
        key_value[:, heads_kv * HEAD_SIZE :].reshape(tok, heads_kv, HEAD_SIZE).astype(jnp.bfloat16)
    )
    paired = jnp.stack([key_rows, value_rows])
    reach = min(n_ctx - 1, -(-(DOC_MOST - 1) // tok))
    blocks = [paired]
    for s in range(1, reach + 1):
        blocks.append(lax.ppermute(paired, "context", [(j, j + s) for j in range(n_ctx - s)]))
    keys_all = jnp.concatenate([b[0] for b in blocks], axis=0)
    values_all = jnp.concatenate([b[1] for b in blocks], axis=0)
    ids = doc_ids[0]
    key_pos = jnp.concatenate(
        [(position - s) * tok + jnp.arange(tok, dtype=jnp.int32) for s in range(reach + 1)]
    )
    key_doc = jnp.take(ids, jnp.clip(key_pos, 0, ids.shape[0] - 1))
    query_doc = lax.dynamic_slice_in_dim(ids, position * tok, tok, 0)
    allowed = (
        (key_pos[None, :] <= query_pos[:, None])
        & (key_pos[None, :] >= 0)
        & (key_doc[None, :] == query_doc[:, None])
    )
    grouped_queries = queries[0].reshape(tok, heads_kv, group, HEAD_SIZE)
    scores = (
        jnp.einsum("qhgd,khd->hgqk", grouped_queries, keys_all, preferred_element_type=jnp.float32)
        * scale
    )
    scores = jnp.where(allowed[None, None], scores, NEG)
    maxima = jnp.max(scores, axis=-1)
    weights = jnp.where(allowed[None, None], jnp.exp(scores - maxima[..., None]), 0.0)
    totals = jnp.sum(weights, axis=-1)
    sums = jnp.einsum(
        "hgqk,khd->hgqd", weights.astype(jnp.bfloat16), values_all, preferred_element_type=jnp.float32
    )
    result = sums / totals[..., None]
    result = (
        jnp.transpose(result, (2, 0, 1, 3)).reshape(tok, heads_q * HEAD_SIZE).astype(jnp.bfloat16)
    )
    return result[None]


def solution(mesh):
    return jax.shard_map(
        functools.partial(shards, mesh.shape["dp"], mesh.shape["context"]),
        mesh=mesh,
        in_specs=(P("dp", "context", None), P("dp", "context", None), P("dp", None), P("dp", None)),
        out_specs=P("dp", "context", None),
        check_vma=False,
    )
```

```python
import functools

import jax
import jax.numpy as jnp
from jax import lax
from jax.sharding import PartitionSpec as P

HEAD_SIZE = 128
DOC_MOST = 1152

NEG = -1e30


def apply_rotation(key_rows, positions):
    half = key_rows.shape[-1] // 2
    freq = 500000.0 ** (-(jnp.arange(half, dtype=jnp.float32) * 2.0 / key_rows.shape[-1]))
    angle = positions.astype(jnp.float32)[:, None] * freq[None, :]
    cosine = jnp.cos(angle)[:, None, :]
    sine = jnp.sin(angle)[:, None, :]
    first = key_rows[..., :half]
    second = key_rows[..., half:]
    return jnp.concatenate(
        [first * cosine - second * sine, second * cosine + first * sine], axis=-1
    )


def exchange(block, axis_name, pairs):
    return lax.ppermute(block, axis_name, pairs)


def gather_rows(block, n_dp):
    nc, ny = 2, 8
    nz = n_dp // (nc * ny)
    index = lax.axis_index("dp")
    z, y, core = index // (ny * nc), (index // nc) % ny, index % nc
    buf = block[None]
    for b in reversed(range(nz.bit_length() - 1)):
        m = (1 << b) * ny * nc
        other = exchange(buf, "dp", [(j, j ^ m) for j in range(n_dp)])
        low_side = ((z >> b) & 1) == 0
        lo = jnp.where(low_side, buf, other)
        hi = jnp.where(low_side, other, buf)
        buf = jnp.concatenate([lo[:, None], hi[:, None]], axis=1).reshape((-1,) + block.shape)

    def along_y(step):
        return [(j, (j // (ny * nc)) * ny * nc + ((j // nc + step) % ny) * nc + j % nc) for j in range(n_dp)]

    forward, backward = buf, buf
    ahead, behind = [], []
    for t in range(1, ny // 2 + 1):
        forward = exchange(forward, "dp", along_y(1))
        behind.append(forward)
    for t in range(1, ny - ny // 2):
        backward = exchange(backward, "dp", along_y(-1))
        ahead.append(backward)
    pieces = jnp.stack([buf] + ahead + behind[::-1])
    pieces = jnp.roll(pieces, y, axis=0)
    other = exchange(pieces, "dp", [(j, j ^ 1) for j in range(n_dp)])
    first = jnp.where(core == 0, pieces, other)
    second = jnp.where(core == 0, other, pieces)
    full = jnp.transpose(jnp.stack([first, second], axis=2), (1, 0, 2, 3, 4))
    return full.reshape((-1,) + block.shape[1:])


def shards(n_dp, n_ctx, hidden_in, queries, kv_weight, doc_ids):
    acts = hidden_in[0]
    tok = acts.shape[0]
    columns = kv_weight.shape[1]
    heads_kv = columns // (2 * HEAD_SIZE)
    heads_q = queries.shape[2] // HEAD_SIZE
    group = heads_q // heads_kv
    scale = 1.0 / float(HEAD_SIZE) ** 0.5
    position = lax.axis_index("context")
    weight = gather_rows(kv_weight, n_dp)
    key_value = jnp.dot(acts, weight, preferred_element_type=jnp.float32)
    query_pos = position * tok + jnp.arange(tok, dtype=jnp.int32)
    key_rows = apply_rotation(
        key_value[:, : heads_kv * HEAD_SIZE].reshape(tok, heads_kv, HEAD_SIZE), query_pos
    ).astype(jnp.bfloat16)
    value_rows = (
        key_value[:, heads_kv * HEAD_SIZE :].reshape(tok, heads_kv, HEAD_SIZE).astype(jnp.bfloat16)
    )
    paired = jnp.stack([key_rows, value_rows])
    reach = min(n_ctx - 1, -(-(DOC_MOST - 1) // tok))
    width = n_ctx // 2
    g, x = position // width, position % width
    relayed = exchange(paired, "context", [(j, width + j) for j in range(width)])
    slots = [(paired, position), (relayed, jnp.where(g == 1, x, -1))]
    for e in range(1, reach - width + 1):
        moved = exchange(relayed, "context", [(width + j, width + j + e) for j in range(width - e)])
        slots.append((moved, jnp.where((g == 1) & (x >= e), x - e, -1)))
    for d in range(1, width):
        send = jnp.where((g == 1) & (x + d >= width), relayed, paired)
        pairs = [(j, j + d) for j in range(width - d)]
        pairs += [(width + j, width + (j + d) % width) for j in range(width)]
        moved = exchange(send, "context", pairs)
        slots.append((moved, jnp.where(x >= d, position - d, jnp.where(g == 1, x - d + width, -1))))
    keys_all = jnp.concatenate([blk[0] for blk, _ in slots], axis=0)
    values_all = jnp.concatenate([blk[1] for blk, _ in slots], axis=0)
    ids = doc_ids[0]
    key_pos = jnp.concatenate(
        [jnp.where(src >= 0, src * tok + jnp.arange(tok, dtype=jnp.int32), -1) for _, src in slots]
    )
    key_doc = jnp.take(ids, jnp.clip(key_pos, 0, ids.shape[0] - 1))
    query_doc = lax.dynamic_slice_in_dim(ids, position * tok, tok, 0)
    allowed = (
        (key_pos[None, :] <= query_pos[:, None])
        & (key_pos[None, :] >= 0)
        & (key_doc[None, :] == query_doc[:, None])
    )
    grouped_queries = queries[0].reshape(tok, heads_kv, group, HEAD_SIZE)
    scores = (
        jnp.einsum("qhgd,khd->hgqk", grouped_queries, keys_all, preferred_element_type=jnp.float32)
        * scale
    )
    scores = jnp.where(allowed[None, None], scores, NEG)
    maxima = jnp.max(scores, axis=-1)
    weights = jnp.where(allowed[None, None], jnp.exp(scores - maxima[..., None]), 0.0)
    totals = jnp.sum(weights, axis=-1)
    sums = jnp.einsum(
        "hgqk,khd->hgqd", weights.astype(jnp.bfloat16), values_all, preferred_element_type=jnp.float32
    )
    result = sums / totals[..., None]
    result = (
        jnp.transpose(result, (2, 0, 1, 3)).reshape(tok, heads_q * HEAD_SIZE).astype(jnp.bfloat16)
    )
    return result[None]


def solution(mesh):
    return jax.shard_map(
        functools.partial(shards, mesh.shape["dp"], mesh.shape["context"]),
        mesh=mesh,
        in_specs=(P("dp", "context", None), P("dp", "context", None), P("dp", None), P("dp", None)),
        out_specs=P("dp", "context", None),
        check_vma=False,
    )
```

```python
import functools

import jax
import jax.numpy as jnp
from jax import lax
from jax.sharding import PartitionSpec as P

HEAD_SIZE = 128
DOC_MOST = 1152

NEG = -1e30


def apply_rotation(key_rows, positions):
    half = key_rows.shape[-1] // 2
    freq = 500000.0 ** (-(jnp.arange(half, dtype=jnp.float32) * 2.0 / key_rows.shape[-1]))
    angle = positions.astype(jnp.float32)[:, None] * freq[None, :]
    cosine = jnp.cos(angle)[:, None, :]
    sine = jnp.sin(angle)[:, None, :]
    first = key_rows[..., :half]
    second = key_rows[..., half:]
    return jnp.concatenate(
        [first * cosine - second * sine, second * cosine + first * sine], axis=-1
    )


def exchange(block, axis_name, pairs):
    return lax.ppermute(block, axis_name, pairs)


def gather_rows(block, n_dp):
    nc, ny = 2, 8
    nz = n_dp // (nc * ny)
    index = lax.axis_index("dp")
    z, y, core = index // (ny * nc), (index // nc) % ny, index % nc
    buf = block[None]
    for b in reversed(range(nz.bit_length() - 1)):
        m = (1 << b) * ny * nc
        other = exchange(buf, "dp", [(j, j ^ m) for j in range(n_dp)])
        low_side = ((z >> b) & 1) == 0
        lo = jnp.where(low_side, buf, other)
        hi = jnp.where(low_side, other, buf)
        buf = jnp.concatenate([lo[:, None], hi[:, None]], axis=1).reshape((-1,) + block.shape)

    def along_y(step):
        return [(j, (j // (ny * nc)) * ny * nc + ((j // nc + step) % ny) * nc + j % nc) for j in range(n_dp)]

    forward, backward = buf, buf
    ahead, behind = [], []
    for t in range(1, ny // 2 + 1):
        forward = exchange(forward, "dp", along_y(1))
        behind.append(forward)
    for t in range(1, ny - ny // 2):
        backward = exchange(backward, "dp", along_y(-1))
        ahead.append(backward)
    pieces = jnp.stack([buf] + ahead + behind[::-1])
    pieces = jnp.roll(pieces, y, axis=0)
    other = exchange(pieces, "dp", [(j, j ^ 1) for j in range(n_dp)])
    first = jnp.where(core == 0, pieces, other)
    second = jnp.where(core == 0, other, pieces)
    full = jnp.transpose(jnp.stack([first, second], axis=2), (1, 0, 2, 3, 4))
    return full.reshape((-1,) + block.shape[1:])


def shards(n_dp, n_ctx, hidden_in, queries, kv_weight, doc_ids):
    acts = hidden_in[0]
    tok = acts.shape[0]
    columns = kv_weight.shape[1]
    heads_kv = columns // (2 * HEAD_SIZE)
    heads_q = queries.shape[2] // HEAD_SIZE
    group = heads_q // heads_kv
    scale = 1.0 / float(HEAD_SIZE) ** 0.5
    position = lax.axis_index("context")
    query_pos = position * tok + jnp.arange(tok, dtype=jnp.int32)
    reach = min(n_ctx - 1, -(-(DOC_MOST - 1) // tok))
    width = n_ctx // 2
    g, x = position // width, position % width
    sources = [position, jnp.where(g == 1, x, -1)]
    sources += [jnp.where((g == 1) & (x >= e), x - e, -1) for e in range(1, reach - width + 1)]
    sources += [
        jnp.where(x >= d, position - d, jnp.where(g == 1, x - d + width, -1)) for d in range(1, width)
    ]
    ids = doc_ids[0]
    key_pos = jnp.concatenate(
        [jnp.where(src >= 0, src * tok + jnp.arange(tok, dtype=jnp.int32), -1) for src in sources]
    )
    key_doc = jnp.take(ids, jnp.clip(key_pos, 0, ids.shape[0] - 1))
    query_doc = lax.dynamic_slice_in_dim(ids, position * tok, tok, 0)
    allowed = (
        (key_pos[None, :] <= query_pos[:, None])
        & (key_pos[None, :] >= 0)
        & (key_doc[None, :] == query_doc[:, None])
    )
    grouped_queries = queries[0].reshape(tok, heads_kv, group, HEAD_SIZE)

    def spread(paired):
        relayed = exchange(paired, "context", [(j, width + j) for j in range(width)])
        slots = [paired, relayed]
        for e in range(1, reach - width + 1):
            pairs = [(width + j, width + j + e) for j in range(width - e)]
            slots.append(exchange(relayed, "context", pairs))
        for d in range(1, width):
            send = jnp.where((g == 1) & (x + d >= width), relayed, paired)
            pairs = [(j, j + d) for j in range(width - d)]
            pairs += [(width + j, width + (j + d) % width) for j in range(width)]
            slots.append(exchange(send, "context", pairs))
        return slots

    def columns_of(heads):
        cols = [h * HEAD_SIZE + c for h in heads for c in range(HEAD_SIZE)]
        cols = jnp.asarray(cols + [heads_kv * HEAD_SIZE + c for c in cols], jnp.int32)
        return jnp.take(kv_weight, cols, axis=1)

    def project(heads, weight):
        key_value = jnp.dot(acts, weight, preferred_element_type=jnp.float32)
        n = len(heads)
        key_rows = apply_rotation(
            key_value[:, : n * HEAD_SIZE].reshape(tok, n, HEAD_SIZE), query_pos
        ).astype(jnp.bfloat16)
        value_rows = key_value[:, n * HEAD_SIZE :].reshape(tok, n, HEAD_SIZE).astype(jnp.bfloat16)
        return jnp.stack([key_rows, value_rows])

    def attend(heads, paired):
        n = len(heads)
        slots = spread(paired)
        keys_all = jnp.concatenate([blk[0] for blk in slots], axis=0)
        values_all = jnp.concatenate([blk[1] for blk in slots], axis=0)
        q = grouped_queries[:, heads[0] : heads[-1] + 1]
        scores = (
            jnp.einsum("qhgd,khd->hgqk", q, keys_all, preferred_element_type=jnp.float32) * scale
        )
        scores = jnp.where(allowed[None, None], scores, NEG)
        maxima = jnp.max(scores, axis=-1)
        weights = jnp.where(allowed[None, None], jnp.exp(scores - maxima[..., None]), 0.0)
        totals = jnp.sum(weights, axis=-1)
        sums = jnp.einsum(
            "hgqk,khd->hgqd",
            weights.astype(jnp.bfloat16),
            values_all,
            preferred_element_type=jnp.float32,
        )
        result = sums / totals[..., None]
        return jnp.transpose(result, (2, 0, 1, 3)).reshape(tok, n * group * HEAD_SIZE)

    half = heads_kv // 2
    first, second = list(range(0, half)), list(range(half, heads_kv))
    weight_first = gather_rows(columns_of(first), n_dp)
    rows_second, paired_first = lax.optimization_barrier(
        (columns_of(second), project(first, weight_first))
    )
    part_first = attend(first, paired_first)
    weight_second = gather_rows(rows_second, n_dp)
    parts = [part_first, attend(second, project(second, weight_second))]
    result = jnp.concatenate(parts, axis=1).astype(jnp.bfloat16)
    return result[None]


def solution(mesh):
    return jax.shard_map(
        functools.partial(shards, mesh.shape["dp"], mesh.shape["context"]),
        mesh=mesh,
        in_specs=(P("dp", "context", None), P("dp", "context", None), P("dp", None), P("dp", None)),
        out_specs=P("dp", "context", None),
        check_vma=False,
    )
```

```python
import functools

import jax
import jax.numpy as jnp
from jax import lax
from jax.sharding import PartitionSpec as P

HEAD_SIZE = 128
DOC_MOST = 1152

NEG = -1e30


def apply_rotation(key_rows, positions):
    half = key_rows.shape[-1] // 2
    freq = 500000.0 ** (-(jnp.arange(half, dtype=jnp.float32) * 2.0 / key_rows.shape[-1]))
    angle = positions.astype(jnp.float32)[:, None] * freq[None, :]
    cosine = jnp.cos(angle)[:, None, :]
    sine = jnp.sin(angle)[:, None, :]
    first = key_rows[..., :half]
    second = key_rows[..., half:]
    return jnp.concatenate(
        [first * cosine - second * sine, second * cosine + first * sine], axis=-1
    )


def exchange(block, axis_name, pairs):
    return lax.ppermute(block, axis_name, pairs)


def gather_rows(block, n_dp):
    nc, ny = 2, 8
    nz = n_dp // (nc * ny)
    index = lax.axis_index("dp")
    z, y, core = index // (ny * nc), (index // nc) % ny, index % nc
    buf = block[None]
    for b in reversed(range(nz.bit_length() - 1)):
        m = (1 << b) * ny * nc
        other = exchange(buf, "dp", [(j, j ^ m) for j in range(n_dp)])
        low_side = ((z >> b) & 1) == 0
        lo = jnp.where(low_side, buf, other)
        hi = jnp.where(low_side, other, buf)
        buf = jnp.concatenate([lo[:, None], hi[:, None]], axis=1).reshape((-1,) + block.shape)

    def along_y(step):
        return [(j, (j // (ny * nc)) * ny * nc + ((j // nc + step) % ny) * nc + j % nc) for j in range(n_dp)]

    forward, backward = buf, buf
    ahead, behind = [], []
    for t in range(1, ny // 2 + 1):
        forward = exchange(forward, "dp", along_y(1))
        behind.append(forward)
    for t in range(1, ny - ny // 2):
        backward = exchange(backward, "dp", along_y(-1))
        ahead.append(backward)
    pieces = jnp.stack([buf] + ahead + behind[::-1])
    pieces = jnp.roll(pieces, y, axis=0)
    other = exchange(pieces, "dp", [(j, j ^ 1) for j in range(n_dp)])
    first = jnp.where(core == 0, pieces, other)
    second = jnp.where(core == 0, other, pieces)
    full = jnp.transpose(jnp.stack([first, second], axis=2), (1, 0, 2, 3, 4))
    return full.reshape((-1,) + block.shape[1:])


def shards(n_dp, n_ctx, hidden_in, queries, kv_weight, doc_ids):
    acts = hidden_in[0]
    tok = acts.shape[0]
    columns = kv_weight.shape[1]
    heads_kv = columns // (2 * HEAD_SIZE)
    heads_q = queries.shape[2] // HEAD_SIZE
    group = heads_q // heads_kv
    scale = 1.0 / float(HEAD_SIZE) ** 0.5
    position = lax.axis_index("context")
    reach = min(n_ctx - 1, -(-(DOC_MOST - 1) // tok))
    width = n_ctx // 2
    g, x = position // width, position % width
    relayed_acts = exchange(acts, "context", [(j, width + j) for j in range(width)])
    weight = gather_rows(kv_weight, n_dp)
    query_pos = position * tok + jnp.arange(tok, dtype=jnp.int32)
    both_pos = jnp.concatenate([query_pos, x * tok + jnp.arange(tok, dtype=jnp.int32)])
    key_value = jnp.dot(
        jnp.concatenate([acts, relayed_acts], axis=0), weight, preferred_element_type=jnp.float32
    )
    key_rows = apply_rotation(
        key_value[:, : heads_kv * HEAD_SIZE].reshape(2 * tok, heads_kv, HEAD_SIZE), both_pos
    ).astype(jnp.bfloat16)
    value_rows = (
        key_value[:, heads_kv * HEAD_SIZE :]
        .reshape(2 * tok, heads_kv, HEAD_SIZE)
        .astype(jnp.bfloat16)
    )
    both = jnp.stack([key_rows, value_rows])
    paired, relayed = both[:, :tok], both[:, tok:]
    slots = [(paired, position), (relayed, jnp.where(g == 1, x, -1))]
    for e in range(1, reach - width + 1):
        moved = exchange(relayed, "context", [(width + j, width + j + e) for j in range(width - e)])
        slots.append((moved, jnp.where((g == 1) & (x >= e), x - e, -1)))
    for d in range(1, width):
        send = jnp.where((g == 1) & (x + d >= width), relayed, paired)
        pairs = [(j, j + d) for j in range(width - d)]
        pairs += [(width + j, width + (j + d) % width) for j in range(width)]
        moved = exchange(send, "context", pairs)
        slots.append((moved, jnp.where(x >= d, position - d, jnp.where(g == 1, x - d + width, -1))))
    keys_all = jnp.concatenate([blk[0] for blk, _ in slots], axis=0)
    values_all = jnp.concatenate([blk[1] for blk, _ in slots], axis=0)
    ids = doc_ids[0]
    key_pos = jnp.concatenate(
        [jnp.where(src >= 0, src * tok + jnp.arange(tok, dtype=jnp.int32), -1) for _, src in slots]
    )
    key_doc = jnp.take(ids, jnp.clip(key_pos, 0, ids.shape[0] - 1))
    query_doc = lax.dynamic_slice_in_dim(ids, position * tok, tok, 0)
    allowed = (
        (key_pos[None, :] <= query_pos[:, None])
        & (key_pos[None, :] >= 0)
        & (key_doc[None, :] == query_doc[:, None])
    )
    grouped_queries = queries[0].reshape(tok, heads_kv, group, HEAD_SIZE)
    scores = (
        jnp.einsum("qhgd,khd->hgqk", grouped_queries, keys_all, preferred_element_type=jnp.float32)
        * scale
    )
    scores = jnp.where(allowed[None, None], scores, NEG)
    maxima = jnp.max(scores, axis=-1)
    weights = jnp.where(allowed[None, None], jnp.exp(scores - maxima[..., None]), 0.0)
    totals = jnp.sum(weights, axis=-1)
    sums = jnp.einsum(
        "hgqk,khd->hgqd", weights.astype(jnp.bfloat16), values_all, preferred_element_type=jnp.float32
    )
    result = sums / totals[..., None]
    result = (
        jnp.transpose(result, (2, 0, 1, 3)).reshape(tok, heads_q * HEAD_SIZE).astype(jnp.bfloat16)
    )
    return result[None]


def solution(mesh):
    return jax.shard_map(
        functools.partial(shards, mesh.shape["dp"], mesh.shape["context"]),
        mesh=mesh,
        in_specs=(P("dp", "context", None), P("dp", "context", None), P("dp", None), P("dp", None)),
        out_specs=P("dp", "context", None),
        check_vma=False,
    )
```

```python
import functools

import jax
import jax.numpy as jnp
from jax import lax
from jax.sharding import PartitionSpec as P

HEAD_SIZE = 128
DOC_MOST = 1152

NEG = -1e30


def apply_rotation(key_rows, positions):
    half = key_rows.shape[-1] // 2
    freq = 500000.0 ** (-(jnp.arange(half, dtype=jnp.float32) * 2.0 / key_rows.shape[-1]))
    angle = positions.astype(jnp.float32)[:, None] * freq[None, :]
    cosine = jnp.cos(angle)[:, None, :]
    sine = jnp.sin(angle)[:, None, :]
    first = key_rows[..., :half]
    second = key_rows[..., half:]
    return jnp.concatenate(
        [first * cosine - second * sine, second * cosine + first * sine], axis=-1
    )


def exchange(block, axis_name, pairs):
    return lax.ppermute(block, axis_name, pairs)


def gather_rows(block, n_dp, after_z):
    nc, ny = 2, 8
    nz = n_dp // (nc * ny)
    index = lax.axis_index("dp")
    z, y, core = index // (ny * nc), (index // nc) % ny, index % nc
    buf = block[None]
    for b in reversed(range(nz.bit_length() - 1)):
        m = (1 << b) * ny * nc
        other = exchange(buf, "dp", [(j, j ^ m) for j in range(n_dp)])
        low_side = ((z >> b) & 1) == 0
        lo = jnp.where(low_side, buf, other)
        hi = jnp.where(low_side, other, buf)
        buf = jnp.concatenate([lo[:, None], hi[:, None]], axis=1).reshape((-1,) + block.shape)

    buf, held = lax.optimization_barrier((buf, after_z[0]))
    sent = exchange(held, after_z[1], after_z[2])

    def along_y(step):
        return [(j, (j // (ny * nc)) * ny * nc + ((j // nc + step) % ny) * nc + j % nc) for j in range(n_dp)]

    forward, backward = buf, buf
    ahead, behind = [], []
    for t in range(1, ny // 2 + 1):
        if t == ny // 2:
            forward, sent = lax.optimization_barrier((forward, sent))
        forward = exchange(forward, "dp", along_y(1))
        behind.append(forward)
    for t in range(1, ny - ny // 2):
        backward = exchange(backward, "dp", along_y(-1))
        ahead.append(backward)
    pieces = jnp.stack([buf] + ahead + behind[::-1])
    pieces = jnp.roll(pieces, y, axis=0)
    other = exchange(pieces, "dp", [(j, j ^ 1) for j in range(n_dp)])
    first = jnp.where(core == 0, pieces, other)
    second = jnp.where(core == 0, other, pieces)
    full = jnp.transpose(jnp.stack([first, second], axis=2), (1, 0, 2, 3, 4))
    return full.reshape((-1,) + block.shape[1:]), sent


def shards(n_dp, n_ctx, hidden_in, queries, kv_weight, doc_ids):
    acts = hidden_in[0]
    tok = acts.shape[0]
    columns = kv_weight.shape[1]
    heads_kv = columns // (2 * HEAD_SIZE)
    heads_q = queries.shape[2] // HEAD_SIZE
    group = heads_q // heads_kv
    scale = 1.0 / float(HEAD_SIZE) ** 0.5
    position = lax.axis_index("context")
    reach = min(n_ctx - 1, -(-(DOC_MOST - 1) // tok))
    width = n_ctx // 2
    g, x = position // width, position % width
    relay = (acts, "context", [(j, width + j) for j in range(width)])
    weight, relayed_acts = gather_rows(kv_weight, n_dp, relay)
    query_pos = position * tok + jnp.arange(tok, dtype=jnp.int32)
    both_pos = jnp.concatenate([query_pos, x * tok + jnp.arange(tok, dtype=jnp.int32)])
    key_value = jnp.dot(
        jnp.concatenate([acts, relayed_acts], axis=0), weight, preferred_element_type=jnp.float32
    )
    key_rows = apply_rotation(
        key_value[:, : heads_kv * HEAD_SIZE].reshape(2 * tok, heads_kv, HEAD_SIZE), both_pos
    ).astype(jnp.bfloat16)
    value_rows = (
        key_value[:, heads_kv * HEAD_SIZE :]
        .reshape(2 * tok, heads_kv, HEAD_SIZE)
        .astype(jnp.bfloat16)
    )
    both = jnp.stack([key_rows, value_rows])
    paired, relayed = both[:, :tok], both[:, tok:]
    slots = [(paired, position), (relayed, jnp.where(g == 1, x, -1))]
    for e in range(1, reach - width + 1):
        moved = exchange(relayed, "context", [(width + j, width + j + e) for j in range(width - e)])
        slots.append((moved, jnp.where((g == 1) & (x >= e), x - e, -1)))
    for d in range(1, width):
        send = jnp.where((g == 1) & (x + d >= width), relayed, paired)
        pairs = [(j, j + d) for j in range(width - d)]
        pairs += [(width + j, width + (j + d) % width) for j in range(width)]
        moved = exchange(send, "context", pairs)
        slots.append((moved, jnp.where(x >= d, position - d, jnp.where(g == 1, x - d + width, -1))))
    keys_all = jnp.concatenate([blk[0] for blk, _ in slots], axis=0)
    values_all = jnp.concatenate([blk[1] for blk, _ in slots], axis=0)
    ids = doc_ids[0]
    key_pos = jnp.concatenate(
        [jnp.where(src >= 0, src * tok + jnp.arange(tok, dtype=jnp.int32), -1) for _, src in slots]
    )
    key_doc = jnp.take(ids, jnp.clip(key_pos, 0, ids.shape[0] - 1))
    query_doc = lax.dynamic_slice_in_dim(ids, position * tok, tok, 0)
    allowed = (
        (key_pos[None, :] <= query_pos[:, None])
        & (key_pos[None, :] >= 0)
        & (key_doc[None, :] == query_doc[:, None])
    )
    grouped_queries = queries[0].reshape(tok, heads_kv, group, HEAD_SIZE)
    scores = (
        jnp.einsum("qhgd,khd->hgqk", grouped_queries, keys_all, preferred_element_type=jnp.float32)
        * scale
    )
    scores = jnp.where(allowed[None, None], scores, NEG)
    maxima = jnp.max(scores, axis=-1)
    weights = jnp.where(allowed[None, None], jnp.exp(scores - maxima[..., None]), 0.0)
    totals = jnp.sum(weights, axis=-1)
    sums = jnp.einsum(
        "hgqk,khd->hgqd", weights.astype(jnp.bfloat16), values_all, preferred_element_type=jnp.float32
    )
    result = sums / totals[..., None]
    result = (
        jnp.transpose(result, (2, 0, 1, 3)).reshape(tok, heads_q * HEAD_SIZE).astype(jnp.bfloat16)
    )
    return result[None]


def solution(mesh):
    return jax.shard_map(
        functools.partial(shards, mesh.shape["dp"], mesh.shape["context"]),
        mesh=mesh,
        in_specs=(P("dp", "context", None), P("dp", "context", None), P("dp", None), P("dp", None)),
        out_specs=P("dp", "context", None),
        check_vma=False,
    )
```

```python
import functools

import jax
import jax.numpy as jnp
from jax import lax
from jax.sharding import PartitionSpec as P

HEAD_SIZE = 128
DOC_MOST = 1152

NEG = -1e30


def apply_rotation(key_rows, positions):
    half = key_rows.shape[-1] // 2
    freq = 500000.0 ** (-(jnp.arange(half, dtype=jnp.float32) * 2.0 / key_rows.shape[-1]))
    angle = positions.astype(jnp.float32)[:, None] * freq[None, :]
    cosine = jnp.cos(angle)[:, None, :]
    sine = jnp.sin(angle)[:, None, :]
    first = key_rows[..., :half]
    second = key_rows[..., half:]
    return jnp.concatenate(
        [first * cosine - second * sine, second * cosine + first * sine], axis=-1
    )


def exchange(block, axis_name, pairs):
    return lax.ppermute(block, axis_name, pairs)


def gather_rows(block, n_dp, after_z):
    nc, ny = 2, 8
    nz = n_dp // (nc * ny)
    index = lax.axis_index("dp")
    z, y, core = index // (ny * nc), (index // nc) % ny, index % nc
    buf = block[None]
    for b in reversed(range(nz.bit_length() - 1)):
        m = (1 << b) * ny * nc
        other = exchange(buf, "dp", [(j, j ^ m) for j in range(n_dp)])
        low_side = ((z >> b) & 1) == 0
        lo = jnp.where(low_side, buf, other)
        hi = jnp.where(low_side, other, buf)
        buf = jnp.concatenate([lo[:, None], hi[:, None]], axis=1).reshape((-1,) + block.shape)

    buf, held = lax.optimization_barrier((buf, after_z[0]))
    sent = exchange(held, after_z[1], after_z[2])

    def along_y(step):
        return [(j, (j // (ny * nc)) * ny * nc + ((j // nc + step) % ny) * nc + j % nc) for j in range(n_dp)]

    forward, backward = buf, buf
    ahead, behind = [], []
    for t in range(1, ny // 2 + 1):
        if t == ny // 2:
            forward, sent = lax.optimization_barrier((forward, sent))
        forward = exchange(forward, "dp", along_y(1))
        behind.append(forward)
    for t in range(1, ny - ny // 2):
        backward = exchange(backward, "dp", along_y(-1))
        ahead.append(backward)
    pieces = jnp.stack([buf] + ahead + behind[::-1])
    pieces = jnp.roll(pieces, y, axis=0)
    other = exchange(pieces, "dp", [(j, j ^ 1) for j in range(n_dp)])
    first = jnp.where(core == 0, pieces, other)
    second = jnp.where(core == 0, other, pieces)
    full = jnp.transpose(jnp.stack([first, second], axis=2), (1, 0, 2, 3, 4))
    return full.reshape((-1,) + block.shape[1:]), sent


def shards(n_dp, n_ctx, hidden_in, queries, kv_weight, doc_ids):
    acts = hidden_in[0]
    tok = acts.shape[0]
    columns = kv_weight.shape[1]
    heads_kv = columns // (2 * HEAD_SIZE)
    heads_q = queries.shape[2] // HEAD_SIZE
    group = heads_q // heads_kv
    scale = 1.0 / float(HEAD_SIZE) ** 0.5
    position = lax.axis_index("context")
    reach = min(n_ctx - 1, -(-(DOC_MOST - 1) // tok))
    width = n_ctx // 2
    g, x = position // width, position % width
    relay = (acts, "context", [(j, width + j) for j in range(width)])
    weight, relayed_acts = gather_rows(kv_weight, n_dp, relay)
    query_pos = position * tok + jnp.arange(tok, dtype=jnp.int32)
    both_pos = jnp.concatenate([query_pos, x * tok + jnp.arange(tok, dtype=jnp.int32)])
    key_value = jnp.dot(
        jnp.concatenate([acts, relayed_acts], axis=0), weight, preferred_element_type=jnp.float32
    )
    key_rows = apply_rotation(
        key_value[:, : heads_kv * HEAD_SIZE].reshape(2 * tok, heads_kv, HEAD_SIZE), both_pos
    ).astype(jnp.bfloat16)
    value_rows = (
        key_value[:, heads_kv * HEAD_SIZE :]
        .reshape(2 * tok, heads_kv, HEAD_SIZE)
        .astype(jnp.bfloat16)
    )
    both = jnp.stack([key_rows, value_rows])
    paired, relayed = both[:, :tok], both[:, tok:]
    slots = [(paired, position), (relayed, jnp.where(g == 1, x, -1))]
    for e in range(1, reach - width + 1):
        moved = exchange(relayed, "context", [(width + j, width + j + e) for j in range(width - e)])
        slots.append((moved, jnp.where((g == 1) & (x >= e), x - e, -1)))
    for d in range(1, width):
        send = jnp.where((g == 1) & (x + d >= width), relayed, paired)
        pairs = [(j, j + d) for j in range(width - d)]
        pairs += [(width + j, width + (j + d) % width) for j in range(width)]
        moved = exchange(send, "context", pairs)
        slots.append((moved, jnp.where(x >= d, position - d, jnp.where(g == 1, x - d + width, -1))))
    keys_all = jnp.concatenate([blk[0] for blk, _ in slots], axis=0)
    values_all = jnp.concatenate([blk[1] for blk, _ in slots], axis=0)
    ids = doc_ids[0]
    key_pos = jnp.concatenate(
        [jnp.where(src >= 0, src * tok + jnp.arange(tok, dtype=jnp.int32), -1) for _, src in slots]
    )
    key_doc = jnp.concatenate(
        [lax.dynamic_slice_in_dim(ids, jnp.maximum(src, 0) * tok, tok, 0) for _, src in slots]
    )
    query_doc = lax.dynamic_slice_in_dim(ids, position * tok, tok, 0)
    allowed = (
        (key_pos[None, :] <= query_pos[:, None])
        & (key_pos[None, :] >= 0)
        & (key_doc[None, :] == query_doc[:, None])
    )
    grouped_queries = queries[0].reshape(tok, heads_kv, group, HEAD_SIZE)
    scores = (
        jnp.einsum("qhgd,khd->hgqk", grouped_queries, keys_all, preferred_element_type=jnp.float32)
        * scale
    )
    scores = jnp.where(allowed[None, None], scores, NEG)
    maxima = jnp.max(scores, axis=-1)
    weights = jnp.where(allowed[None, None], jnp.exp(scores - maxima[..., None]), 0.0)
    totals = jnp.sum(weights, axis=-1)
    sums = jnp.einsum(
        "hgqk,khd->qhgd", weights.astype(jnp.bfloat16), values_all, preferred_element_type=jnp.float32
    )
    result = sums / jnp.transpose(totals, (2, 0, 1))[..., None]
    result = result.reshape(tok, heads_q * HEAD_SIZE).astype(jnp.bfloat16)
    return result[None]


def solution(mesh):
    return jax.shard_map(
        functools.partial(shards, mesh.shape["dp"], mesh.shape["context"]),
        mesh=mesh,
        in_specs=(P("dp", "context", None), P("dp", "context", None), P("dp", None), P("dp", None)),
        out_specs=P("dp", "context", None),
        check_vma=False,
    )
```

```python
import functools

import jax
import jax.numpy as jnp
from jax import lax
from jax.sharding import PartitionSpec as P

HEAD_SIZE = 128
DOC_MOST = 1152

NEG = -1e30


def apply_rotation(key_rows, positions):
    half = key_rows.shape[-1] // 2
    freq = 500000.0 ** (-(jnp.arange(half, dtype=jnp.float32) * 2.0 / key_rows.shape[-1]))
    angle = positions.astype(jnp.float32)[:, None] * freq[None, :]
    cosine = jnp.cos(angle)[:, None, :]
    sine = jnp.sin(angle)[:, None, :]
    first = key_rows[..., :half]
    second = key_rows[..., half:]
    return jnp.concatenate(
        [first * cosine - second * sine, second * cosine + first * sine], axis=-1
    )


def exchange(block, axis_name, pairs):
    return lax.ppermute(block, axis_name, pairs)


def gather_rows(block, n_dp, after_z):
    nc, ny = 2, 8
    nz = n_dp // (nc * ny)
    index = lax.axis_index("dp")
    z, y, core = index // (ny * nc), (index // nc) % ny, index % nc
    buf = block[None]
    for b in reversed(range(nz.bit_length() - 1)):
        m = (1 << b) * ny * nc
        other = exchange(buf, "dp", [(j, j ^ m) for j in range(n_dp)])
        low_side = ((z >> b) & 1) == 0
        lo = jnp.where(low_side, buf, other)
        hi = jnp.where(low_side, other, buf)
        buf = jnp.concatenate([lo[:, None], hi[:, None]], axis=1).reshape((-1,) + block.shape)

    buf, held = lax.optimization_barrier((buf, after_z[0]))
    sent = exchange(held, after_z[1], after_z[2])

    def along_y(step):
        return [(j, (j // (ny * nc)) * ny * nc + ((j // nc + step) % ny) * nc + j % nc) for j in range(n_dp)]

    forward, backward = buf, buf
    ahead, behind = [], []
    for t in range(1, ny // 2 + 1):
        if t == ny // 2:
            forward, sent = lax.optimization_barrier((forward, sent))
        forward = exchange(forward, "dp", along_y(1))
        behind.append(forward)
    for t in range(1, ny - ny // 2):
        backward = exchange(backward, "dp", along_y(-1))
        ahead.append(backward)
    pieces = jnp.stack([buf] + ahead + behind[::-1])
    pieces = jnp.roll(pieces, y, axis=0)
    other = exchange(pieces, "dp", [(j, j ^ 1) for j in range(n_dp)])
    first = jnp.where(core == 0, pieces, other)
    second = jnp.where(core == 0, other, pieces)
    full = jnp.transpose(jnp.stack([first, second], axis=2), (1, 0, 2, 3, 4))
    return full.reshape((-1,) + block.shape[1:]), sent


def shards(n_dp, n_ctx, hidden_in, queries, kv_weight, doc_ids):
    acts = hidden_in[0]
    tok = acts.shape[0]
    columns = kv_weight.shape[1]
    heads_kv = columns // (2 * HEAD_SIZE)
    heads_q = queries.shape[2] // HEAD_SIZE
    group = heads_q // heads_kv
    scale = 1.0 / float(HEAD_SIZE) ** 0.5
    position = lax.axis_index("context")
    reach = min(n_ctx - 1, -(-(DOC_MOST - 1) // tok))
    width = n_ctx // 2
    g, x = position // width, position % width
    relay = (acts, "context", [(j, width + j) for j in range(width)])
    weight, relayed_acts = gather_rows(kv_weight, n_dp, relay)
    query_pos = position * tok + jnp.arange(tok, dtype=jnp.int32)
    both_pos = jnp.concatenate([query_pos, x * tok + jnp.arange(tok, dtype=jnp.int32)])
    key_value = jnp.dot(
        jnp.concatenate([acts, relayed_acts], axis=0), weight, preferred_element_type=jnp.float32
    )
    key_rows = apply_rotation(
        key_value[:, : heads_kv * HEAD_SIZE].reshape(2 * tok, heads_kv, HEAD_SIZE), both_pos
    ).astype(jnp.bfloat16)
    value_rows = (
        key_value[:, heads_kv * HEAD_SIZE :]
        .reshape(2 * tok, heads_kv, HEAD_SIZE)
        .astype(jnp.bfloat16)
    )
    both = jnp.stack([key_rows, value_rows])
    paired, relayed = both[:, :tok], both[:, tok:]
    slots = [(paired, position), (relayed, jnp.where(g == 1, x, -1))]
    for e in range(1, reach - width + 1):
        moved = exchange(relayed, "context", [(width + j, width + j + e) for j in range(width - e)])
        slots.append((moved, jnp.where((g == 1) & (x >= e), x - e, -1)))
    for d in range(1, width):
        send = jnp.where((g == 1) & (x + d >= width), relayed, paired)
        pairs = [(j, j + d) for j in range(width - d)]
        pairs += [(width + j, width + (j + d) % width) for j in range(width)]
        moved = exchange(send, "context", pairs)
        slots.append((moved, jnp.where(x >= d, position - d, jnp.where(g == 1, x - d + width, -1))))
    ids = doc_ids[0]
    query_doc = lax.dynamic_slice_in_dim(ids, position * tok, tok, 0)
    grouped_queries = queries[0].reshape(tok, heads_kv, group, HEAD_SIZE)
    maxima = jnp.full((heads_kv, group, tok), NEG, jnp.float32)
    totals = jnp.zeros((heads_kv, group, tok), jnp.float32)
    sums = jnp.zeros((tok, heads_kv, group, HEAD_SIZE), jnp.float32)
    for blk, src in slots:
        key_pos = jnp.where(src >= 0, src * tok + jnp.arange(tok, dtype=jnp.int32), -1)
        key_doc = lax.dynamic_slice_in_dim(ids, jnp.maximum(src, 0) * tok, tok, 0)
        allowed = (
            (key_pos[None, :] <= query_pos[:, None])
            & (key_pos[None, :] >= 0)
            & (key_doc[None, :] == query_doc[:, None])
        )
        scores = (
            jnp.einsum("qhgd,khd->hgqk", grouped_queries, blk[0], preferred_element_type=jnp.float32)
            * scale
        )
        scores = jnp.where(allowed[None, None], scores, NEG)
        fresh = jnp.maximum(maxima, jnp.max(scores, axis=-1))
        kept = jnp.exp(maxima - fresh)
        weights = jnp.where(allowed[None, None], jnp.exp(scores - fresh[..., None]), 0.0)
        totals = totals * kept + jnp.sum(weights, axis=-1)
        added = jnp.einsum(
            "hgqk,khd->qhgd", weights.astype(jnp.bfloat16), blk[1], preferred_element_type=jnp.float32
        )
        sums = sums * jnp.transpose(kept, (2, 0, 1))[..., None] + added
        maxima = fresh
    result = sums / jnp.transpose(totals, (2, 0, 1))[..., None]
    result = result.reshape(tok, heads_q * HEAD_SIZE).astype(jnp.bfloat16)
    return result[None]


def solution(mesh):
    return jax.shard_map(
        functools.partial(shards, mesh.shape["dp"], mesh.shape["context"]),
        mesh=mesh,
        in_specs=(P("dp", "context", None), P("dp", "context", None), P("dp", None), P("dp", None)),
        out_specs=P("dp", "context", None),
        check_vma=False,
    )
```

```python
import functools

import jax
import jax.numpy as jnp
from jax import lax
from jax.sharding import PartitionSpec as P

HEAD_SIZE = 128
DOC_MOST = 1152

NEG = -1e30


def apply_rotation(key_rows, positions):
    half = key_rows.shape[-1] // 2
    freq = 500000.0 ** (-(jnp.arange(half, dtype=jnp.float32) * 2.0 / key_rows.shape[-1]))
    angle = positions.astype(jnp.float32)[:, None] * freq[None, :]
    cosine = jnp.cos(angle)[:, None, :]
    sine = jnp.sin(angle)[:, None, :]
    first = key_rows[..., :half]
    second = key_rows[..., half:]
    return jnp.concatenate(
        [first * cosine - second * sine, second * cosine + first * sine], axis=-1
    )


def exchange(block, axis_name, pairs):
    return lax.ppermute(block, axis_name, pairs)


def gather_rows(block, n_dp, after_z):
    nc, ny = 2, 8
    nz = n_dp // (nc * ny)
    index = lax.axis_index("dp")
    z, y, core = index // (ny * nc), (index // nc) % ny, index % nc
    buf = block[None]
    for b in reversed(range(nz.bit_length() - 1)):
        m = (1 << b) * ny * nc
        other = exchange(buf, "dp", [(j, j ^ m) for j in range(n_dp)])
        low_side = ((z >> b) & 1) == 0
        lo = jnp.where(low_side, buf, other)
        hi = jnp.where(low_side, other, buf)
        buf = jnp.concatenate([lo[:, None], hi[:, None]], axis=1).reshape((-1,) + block.shape)

    buf, held = lax.optimization_barrier((buf, after_z[0]))
    sent = exchange(held, after_z[1], after_z[2])

    def along_y(step):
        return [(j, (j // (ny * nc)) * ny * nc + ((j // nc + step) % ny) * nc + j % nc) for j in range(n_dp)]

    forward, backward = buf, buf
    ahead, behind = [], []
    for t in range(1, ny // 2 + 1):
        if t == ny // 2:
            forward, sent = lax.optimization_barrier((forward, sent))
        forward = exchange(forward, "dp", along_y(1))
        behind.append(forward)
    for t in range(1, ny - ny // 2):
        backward = exchange(backward, "dp", along_y(-1))
        ahead.append(backward)
    pieces = jnp.stack([buf] + ahead + behind[::-1])
    pieces = jnp.roll(pieces, y, axis=0)
    other = exchange(pieces, "dp", [(j, j ^ 1) for j in range(n_dp)])
    first = jnp.where(core == 0, pieces, other)
    second = jnp.where(core == 0, other, pieces)
    full = jnp.transpose(jnp.stack([first, second], axis=2), (1, 0, 2, 3, 4))
    return full.reshape((-1,) + block.shape[1:]), sent


def shards(n_dp, n_ctx, hidden_in, queries, kv_weight, doc_ids):
    acts = hidden_in[0]
    tok = acts.shape[0]
    columns = kv_weight.shape[1]
    heads_kv = columns // (2 * HEAD_SIZE)
    heads_q = queries.shape[2] // HEAD_SIZE
    group = heads_q // heads_kv
    scale = 1.0 / float(HEAD_SIZE) ** 0.5
    position = lax.axis_index("context")
    reach = min(n_ctx - 1, -(-(DOC_MOST - 1) // tok))
    width = n_ctx // 2
    g, x = position // width, position % width
    relay = (acts, "context", [(j, width + j) for j in range(width)])
    weight, relayed_acts = gather_rows(kv_weight, n_dp, relay)
    query_pos = position * tok + jnp.arange(tok, dtype=jnp.int32)
    both_pos = jnp.concatenate([query_pos, x * tok + jnp.arange(tok, dtype=jnp.int32)])
    key_value = jnp.dot(
        jnp.concatenate([acts, relayed_acts], axis=0), weight, preferred_element_type=jnp.float32
    )
    key_rows = apply_rotation(
        key_value[:, : heads_kv * HEAD_SIZE].reshape(2 * tok, heads_kv, HEAD_SIZE), both_pos
    ).astype(jnp.bfloat16)
    value_rows = (
        key_value[:, heads_kv * HEAD_SIZE :]
        .reshape(2 * tok, heads_kv, HEAD_SIZE)
        .astype(jnp.bfloat16)
    )
    both = jnp.stack([key_rows, value_rows])
    paired, relayed = both[:, :tok], both[:, tok:]
    slots = [(paired, position), (relayed, jnp.where(g == 1, x, -1))]
    for e in range(1, reach - width + 1):
        moved = exchange(relayed, "context", [(width + j, width + j + e) for j in range(width - e)])
        slots.append((moved, jnp.where((g == 1) & (x >= e), x - e, -1)))
    for d in range(1, width):
        send = jnp.where((g == 1) & (x + d >= width), relayed, paired)
        pairs = [(j, j + d) for j in range(width - d)]
        pairs += [(width + j, width + (j + d) % width) for j in range(width)]
        moved = exchange(send, "context", pairs)
        slots.append((moved, jnp.where(x >= d, position - d, jnp.where(g == 1, x - d + width, -1))))
    keys_all = jnp.concatenate([blk[0] for blk, _ in slots], axis=0)
    values_all = jnp.concatenate([blk[1] for blk, _ in slots], axis=0)
    ids = doc_ids[0]
    key_pos = jnp.concatenate(
        [jnp.where(src >= 0, src * tok + jnp.arange(tok, dtype=jnp.int32), -1) for _, src in slots]
    )
    key_doc = jnp.concatenate(
        [lax.dynamic_slice_in_dim(ids, jnp.maximum(src, 0) * tok, tok, 0) for _, src in slots]
    )
    query_doc = lax.dynamic_slice_in_dim(ids, position * tok, tok, 0)
    allowed = (
        (key_pos[None, :] <= query_pos[:, None])
        & (key_pos[None, :] >= 0)
        & (key_doc[None, :] == query_doc[:, None])
    )
    rows = group * tok
    stacked_queries = jnp.transpose(
        queries[0].reshape(tok, heads_kv, group, HEAD_SIZE), (1, 2, 0, 3)
    ).reshape(heads_kv, rows, HEAD_SIZE)
    wide_allowed = jnp.broadcast_to(allowed[None], (group,) + allowed.shape).reshape(1, rows, -1)
    scores = (
        jnp.einsum("hmd,khd->hmk", stacked_queries, keys_all, preferred_element_type=jnp.float32)
        * scale
    )
    scores = jnp.where(wide_allowed, scores, NEG)
    maxima = jnp.max(scores, axis=-1)
    weights = jnp.where(wide_allowed, jnp.exp(scores - maxima[..., None]), 0.0)
    totals = jnp.sum(weights, axis=-1)
    sums = jnp.einsum(
        "hmk,khd->hmd", weights.astype(jnp.bfloat16), values_all, preferred_element_type=jnp.float32
    )
    result = (sums / totals[..., None]).astype(jnp.bfloat16)
    result = jnp.transpose(result.reshape(heads_kv, group, tok, HEAD_SIZE), (2, 0, 1, 3))
    result = result.reshape(tok, heads_q * HEAD_SIZE)
    return result[None]


def solution(mesh):
    return jax.shard_map(
        functools.partial(shards, mesh.shape["dp"], mesh.shape["context"]),
        mesh=mesh,
        in_specs=(P("dp", "context", None), P("dp", "context", None), P("dp", None), P("dp", None)),
        out_specs=P("dp", "context", None),
        check_vma=False,
    )
```

```python
import functools

import jax
import jax.numpy as jnp
from jax import lax
from jax.sharding import PartitionSpec as P

HEAD_SIZE = 128
DOC_MOST = 1152

NEG = -1e30


def apply_rotation(key_rows, positions):
    half = key_rows.shape[-1] // 2
    freq = 500000.0 ** (-(jnp.arange(half, dtype=jnp.float32) * 2.0 / key_rows.shape[-1]))
    angle = positions.astype(jnp.float32)[:, None] * freq[None, :]
    cosine = jnp.cos(angle)[:, None, :]
    sine = jnp.sin(angle)[:, None, :]
    first = key_rows[..., :half]
    second = key_rows[..., half:]
    return jnp.concatenate(
        [first * cosine - second * sine, second * cosine + first * sine], axis=-1
    )


def exchange(block, axis_name, pairs):
    return lax.ppermute(block, axis_name, pairs)


def gather_rows(block, n_dp, after_z):
    nc, ny = 2, 8
    nz = n_dp // (nc * ny)
    index = lax.axis_index("dp")
    z, y, core = index // (ny * nc), (index // nc) % ny, index % nc
    buf = block[None]
    for b in reversed(range(nz.bit_length() - 1)):
        m = (1 << b) * ny * nc
        other = exchange(buf, "dp", [(j, j ^ m) for j in range(n_dp)])
        low_side = ((z >> b) & 1) == 0
        lo = jnp.where(low_side, buf, other)
        hi = jnp.where(low_side, other, buf)
        buf = jnp.concatenate([lo[:, None], hi[:, None]], axis=1).reshape((-1,) + block.shape)

    buf, held = lax.optimization_barrier((buf, after_z[0]))
    sent = exchange(held, after_z[1], after_z[2])

    def along_y(step):
        return [(j, (j // (ny * nc)) * ny * nc + ((j // nc + step) % ny) * nc + j % nc) for j in range(n_dp)]

    forward, backward = buf, buf
    ahead, behind = [], []
    for t in range(1, ny // 2 + 1):
        forward = exchange(forward, "dp", along_y(1))
        behind.append(forward)
    for t in range(1, ny - ny // 2):
        backward = exchange(backward, "dp", along_y(-1))
        ahead.append(backward)
    pieces = jnp.stack([buf] + ahead + behind[::-1])
    pieces, sent = lax.optimization_barrier((pieces, sent))
    pieces = jnp.roll(pieces, y, axis=0)
    other = exchange(pieces, "dp", [(j, j ^ 1) for j in range(n_dp)])
    first = jnp.where(core == 0, pieces, other)
    second = jnp.where(core == 0, other, pieces)
    full = jnp.transpose(jnp.stack([first, second], axis=2), (1, 0, 2, 3, 4))
    return full.reshape((-1,) + block.shape[1:]), sent


def shards(n_dp, n_ctx, hidden_in, queries, kv_weight, doc_ids):
    acts = hidden_in[0]
    tok = acts.shape[0]
    columns = kv_weight.shape[1]
    heads_kv = columns // (2 * HEAD_SIZE)
    heads_q = queries.shape[2] // HEAD_SIZE
    group = heads_q // heads_kv
    scale = 1.0 / float(HEAD_SIZE) ** 0.5
    position = lax.axis_index("context")
    reach = min(n_ctx - 1, -(-(DOC_MOST - 1) // tok))
    width = n_ctx // 2
    g, x = position // width, position % width
    relay = (acts, "context", [(j, width + j) for j in range(width)])
    weight, relayed_acts = gather_rows(kv_weight, n_dp, relay)
    query_pos = position * tok + jnp.arange(tok, dtype=jnp.int32)
    both_pos = jnp.concatenate([query_pos, x * tok + jnp.arange(tok, dtype=jnp.int32)])
    key_value = jnp.dot(
        jnp.concatenate([acts, relayed_acts], axis=0), weight, preferred_element_type=jnp.float32
    )
    key_rows = apply_rotation(
        key_value[:, : heads_kv * HEAD_SIZE].reshape(2 * tok, heads_kv, HEAD_SIZE), both_pos
    ).astype(jnp.bfloat16)
    value_rows = (
        key_value[:, heads_kv * HEAD_SIZE :]
        .reshape(2 * tok, heads_kv, HEAD_SIZE)
        .astype(jnp.bfloat16)
    )
    both = jnp.stack([key_rows, value_rows])
    paired, relayed = both[:, :tok], both[:, tok:]
    slots = [(paired, position), (relayed, jnp.where(g == 1, x, -1))]
    for e in range(1, reach - width + 1):
        moved = exchange(relayed, "context", [(width + j, width + j + e) for j in range(width - e)])
        slots.append((moved, jnp.where((g == 1) & (x >= e), x - e, -1)))
    for d in range(1, width):
        send = jnp.where((g == 1) & (x + d >= width), relayed, paired)
        pairs = [(j, j + d) for j in range(width - d)]
        pairs += [(width + j, width + (j + d) % width) for j in range(width)]
        moved = exchange(send, "context", pairs)
        slots.append((moved, jnp.where(x >= d, position - d, jnp.where(g == 1, x - d + width, -1))))
    keys_all = jnp.concatenate([blk[0] for blk, _ in slots], axis=0)
    values_all = jnp.concatenate([blk[1] for blk, _ in slots], axis=0)
    ids = doc_ids[0]
    key_pos = jnp.concatenate(
        [jnp.where(src >= 0, src * tok + jnp.arange(tok, dtype=jnp.int32), -1) for _, src in slots]
    )
    key_doc = jnp.concatenate(
        [lax.dynamic_slice_in_dim(ids, jnp.maximum(src, 0) * tok, tok, 0) for _, src in slots]
    )
    query_doc = lax.dynamic_slice_in_dim(ids, position * tok, tok, 0)
    allowed = (
        (key_pos[None, :] <= query_pos[:, None])
        & (key_pos[None, :] >= 0)
        & (key_doc[None, :] == query_doc[:, None])
    )
    grouped_queries = queries[0].reshape(tok, heads_kv, group, HEAD_SIZE)
    scores = (
        jnp.einsum("qhgd,khd->hgqk", grouped_queries, keys_all, preferred_element_type=jnp.float32)
        * scale
    )
    scores = jnp.where(allowed[None, None], scores, NEG)
    maxima = jnp.max(scores, axis=-1)
    weights = jnp.where(allowed[None, None], jnp.exp(scores - maxima[..., None]), 0.0)
    totals = jnp.sum(weights, axis=-1)
    sums = jnp.einsum(
        "hgqk,khd->qhgd", weights.astype(jnp.bfloat16), values_all, preferred_element_type=jnp.float32
    )
    result = sums / jnp.transpose(totals, (2, 0, 1))[..., None]
    result = result.reshape(tok, heads_q * HEAD_SIZE).astype(jnp.bfloat16)
    return result[None]


def solution(mesh):
    return jax.shard_map(
        functools.partial(shards, mesh.shape["dp"], mesh.shape["context"]),
        mesh=mesh,
        in_specs=(P("dp", "context", None), P("dp", "context", None), P("dp", None), P("dp", None)),
        out_specs=P("dp", "context", None),
        check_vma=False,
    )
```

```python
import functools

import jax
import jax.numpy as jnp
from jax import lax
from jax.sharding import PartitionSpec as P

HEAD_SIZE = 128
DOC_MOST = 1152

NEG = -1e30


def apply_rotation(key_rows, positions):
    half = key_rows.shape[-1] // 2
    freq = 500000.0 ** (-(jnp.arange(half, dtype=jnp.float32) * 2.0 / key_rows.shape[-1]))
    angle = positions.astype(jnp.float32)[:, None] * freq[None, :]
    cosine = jnp.cos(angle)[:, None, :]
    sine = jnp.sin(angle)[:, None, :]
    first = key_rows[..., :half]
    second = key_rows[..., half:]
    return jnp.concatenate(
        [first * cosine - second * sine, second * cosine + first * sine], axis=-1
    )


def exchange(block, axis_name, pairs):
    return lax.ppermute(block, axis_name, pairs)


def gather_rows(block, n_dp, after_z):
    nc, ny = 2, 8
    nz = n_dp // (nc * ny)
    index = lax.axis_index("dp")
    z, y, core = index // (ny * nc), (index // nc) % ny, index % nc
    buf = block[None]
    for b in reversed(range(nz.bit_length() - 1)):
        m = (1 << b) * ny * nc
        other = exchange(buf, "dp", [(j, j ^ m) for j in range(n_dp)])
        low_side = ((z >> b) & 1) == 0
        lo = jnp.where(low_side, buf, other)
        hi = jnp.where(low_side, other, buf)
        buf = jnp.concatenate([lo[:, None], hi[:, None]], axis=1).reshape((-1,) + block.shape)

    buf, held = lax.optimization_barrier((buf, after_z[0]))
    sent = exchange(held, after_z[1], after_z[2])

    def along_y(step):
        return [(j, (j // (ny * nc)) * ny * nc + ((j // nc + step) % ny) * nc + j % nc) for j in range(n_dp)]

    forward, backward = buf, buf
    ahead, behind = [], []
    for t in range(1, ny // 2 + 1):
        forward = exchange(forward, "dp", along_y(1))
        behind.append(forward)
    for t in range(1, ny - ny // 2):
        backward = exchange(backward, "dp", along_y(-1))
        ahead.append(backward)
    pieces = jnp.stack([buf] + ahead + behind[::-1])
    pieces, sent = lax.optimization_barrier((pieces, sent))
    pieces = jnp.roll(pieces, y, axis=0)
    other = exchange(pieces, "dp", [(j, j ^ 1) for j in range(n_dp)])
    first = jnp.where(core == 0, pieces, other)
    second = jnp.where(core == 0, other, pieces)
    full = jnp.transpose(jnp.stack([first, second], axis=2), (1, 0, 2, 3, 4))
    return full.reshape((-1,) + block.shape[1:]), sent


def shards(n_dp, n_ctx, hidden_in, queries, kv_weight, doc_ids):
    acts = hidden_in[0]
    tok = acts.shape[0]
    columns = kv_weight.shape[1]
    heads_kv = columns // (2 * HEAD_SIZE)
    heads_q = queries.shape[2] // HEAD_SIZE
    group = heads_q // heads_kv
    scale = 1.0 / float(HEAD_SIZE) ** 0.5
    position = lax.axis_index("context")
    reach = min(n_ctx - 1, -(-(DOC_MOST - 1) // tok))
    width = n_ctx // 2
    g, x = position // width, position % width
    relay = (acts, "context", [(j, width + j) for j in range(width)])
    weight, relayed_acts = gather_rows(kv_weight, n_dp, relay)
    query_pos = position * tok + jnp.arange(tok, dtype=jnp.int32)
    both_pos = jnp.concatenate([query_pos, x * tok + jnp.arange(tok, dtype=jnp.int32)])
    key_value = jnp.dot(
        jnp.concatenate([acts, relayed_acts], axis=0), weight, preferred_element_type=jnp.float32
    )
    key_rows = apply_rotation(
        key_value[:, : heads_kv * HEAD_SIZE].reshape(2 * tok, heads_kv, HEAD_SIZE), both_pos
    ).astype(jnp.bfloat16)
    value_rows = (
        key_value[:, heads_kv * HEAD_SIZE :]
        .reshape(2 * tok, heads_kv, HEAD_SIZE)
        .astype(jnp.bfloat16)
    )
    both = jnp.stack([key_rows, value_rows])
    paired, relayed = both[:, :tok], both[:, tok:]
    slots = [(paired, position), (relayed, jnp.where(g == 1, x, -1))]
    for d in sorted(range(1, width), key=lambda d: (-min(d, width - d), d)):
        send = jnp.where((g == 1) & (x + d >= width), relayed, paired)
        pairs = [(j, j + d) for j in range(width - d)]
        pairs += [(width + j, width + (j + d) % width) for j in range(width)]
        moved = exchange(send, "context", pairs)
        slots.append((moved, jnp.where(x >= d, position - d, jnp.where(g == 1, x - d + width, -1))))
    for e in range(1, reach - width + 1):
        moved = exchange(relayed, "context", [(width + j, width + j + e) for j in range(width - e)])
        slots.append((moved, jnp.where((g == 1) & (x >= e), x - e, -1)))
    keys_all = jnp.concatenate([blk[0] for blk, _ in slots], axis=0)
    values_all = jnp.concatenate([blk[1] for blk, _ in slots], axis=0)
    ids = doc_ids[0]
    key_pos = jnp.concatenate(
        [jnp.where(src >= 0, src * tok + jnp.arange(tok, dtype=jnp.int32), -1) for _, src in slots]
    )
    key_doc = jnp.concatenate(
        [lax.dynamic_slice_in_dim(ids, jnp.maximum(src, 0) * tok, tok, 0) for _, src in slots]
    )
    query_doc = lax.dynamic_slice_in_dim(ids, position * tok, tok, 0)
    allowed = (
        (key_pos[None, :] <= query_pos[:, None])
        & (key_pos[None, :] >= 0)
        & (key_doc[None, :] == query_doc[:, None])
    )
    grouped_queries = queries[0].reshape(tok, heads_kv, group, HEAD_SIZE)
    scores = (
        jnp.einsum("qhgd,khd->hgqk", grouped_queries, keys_all, preferred_element_type=jnp.float32)
        * scale
    )
    scores = jnp.where(allowed[None, None], scores, NEG)
    maxima = jnp.max(scores, axis=-1)
    weights = jnp.where(allowed[None, None], jnp.exp(scores - maxima[..., None]), 0.0)
    totals = jnp.sum(weights, axis=-1)
    sums = jnp.einsum(
        "hgqk,khd->qhgd", weights.astype(jnp.bfloat16), values_all, preferred_element_type=jnp.float32
    )
    result = sums / jnp.transpose(totals, (2, 0, 1))[..., None]
    result = result.reshape(tok, heads_q * HEAD_SIZE).astype(jnp.bfloat16)
    return result[None]


def solution(mesh):
    return jax.shard_map(
        functools.partial(shards, mesh.shape["dp"], mesh.shape["context"]),
        mesh=mesh,
        in_specs=(P("dp", "context", None), P("dp", "context", None), P("dp", None), P("dp", None)),
        out_specs=P("dp", "context", None),
        check_vma=False,
    )
```

```python
import functools

import jax
import jax.numpy as jnp
from jax import lax
from jax.sharding import PartitionSpec as P

HEAD_SIZE = 128
DOC_MOST = 1152

NEG = -1e30


def apply_rotation(key_rows, positions):
    half = key_rows.shape[-1] // 2
    freq = 500000.0 ** (-(jnp.arange(half, dtype=jnp.float32) * 2.0 / key_rows.shape[-1]))
    angle = positions.astype(jnp.float32)[:, None] * freq[None, :]
    cosine = jnp.cos(angle)[:, None, :]
    sine = jnp.sin(angle)[:, None, :]
    first = key_rows[..., :half]
    second = key_rows[..., half:]
    return jnp.concatenate(
        [first * cosine - second * sine, second * cosine + first * sine], axis=-1
    )


def exchange(block, axis_name, pairs):
    return lax.ppermute(block, axis_name, pairs)


def gather_rows(block, n_dp, after_z):
    nc, ny = 2, 8
    nz = n_dp // (nc * ny)
    index = lax.axis_index("dp")
    z, y, core = index // (ny * nc), (index // nc) % ny, index % nc
    buf = block[None]
    for b in reversed(range(nz.bit_length() - 1)):
        m = (1 << b) * ny * nc
        other = exchange(buf, "dp", [(j, j ^ m) for j in range(n_dp)])
        low_side = ((z >> b) & 1) == 0
        lo = jnp.where(low_side, buf, other)
        hi = jnp.where(low_side, other, buf)
        buf = jnp.concatenate([lo[:, None], hi[:, None]], axis=1).reshape((-1,) + block.shape)

    buf, held = lax.optimization_barrier((buf, after_z[0]))
    sent = exchange(held, after_z[1], after_z[2])

    def along_y(step):
        return [(j, (j // (ny * nc)) * ny * nc + ((j // nc + step) % ny) * nc + j % nc) for j in range(n_dp)]

    forward, backward = buf, buf
    ahead, behind = [], []
    for t in range(1, ny // 2 + 1):
        forward = exchange(forward, "dp", along_y(1))
        behind.append(forward)
    for t in range(1, ny - ny // 2):
        backward = exchange(backward, "dp", along_y(-1))
        ahead.append(backward)
    pieces = jnp.stack([buf] + ahead + behind[::-1])
    pieces, sent = lax.optimization_barrier((pieces, sent))
    pieces = jnp.roll(pieces, y, axis=0)
    other = exchange(pieces, "dp", [(j, j ^ 1) for j in range(n_dp)])
    first = jnp.where(core == 0, pieces, other)
    second = jnp.where(core == 0, other, pieces)
    full = jnp.transpose(jnp.stack([first, second], axis=2), (1, 0, 2, 3, 4))
    return full.reshape((-1,) + block.shape[1:]), sent


def shards(n_dp, n_ctx, hidden_in, queries, kv_weight, doc_ids):
    acts = hidden_in[0]
    tok = acts.shape[0]
    columns = kv_weight.shape[1]
    heads_kv = columns // (2 * HEAD_SIZE)
    heads_q = queries.shape[2] // HEAD_SIZE
    group = heads_q // heads_kv
    scale = 1.0 / float(HEAD_SIZE) ** 0.5
    position = lax.axis_index("context")
    reach = min(n_ctx - 1, -(-(DOC_MOST - 1) // tok))
    width = n_ctx // 2
    g, x = position // width, position % width
    relay = (acts, "context", [(j, width + j) for j in range(width)])
    weight, relayed_acts = gather_rows(kv_weight, n_dp, relay)
    query_pos = position * tok + jnp.arange(tok, dtype=jnp.int32)
    both_pos = jnp.concatenate([query_pos, x * tok + jnp.arange(tok, dtype=jnp.int32)])
    key_value = jnp.dot(
        jnp.concatenate([acts, relayed_acts], axis=0), weight, preferred_element_type=jnp.float32
    )
    key_rows = apply_rotation(
        key_value[:, : heads_kv * HEAD_SIZE].reshape(2 * tok, heads_kv, HEAD_SIZE), both_pos
    ).astype(jnp.bfloat16)
    value_rows = (
        key_value[:, heads_kv * HEAD_SIZE :]
        .reshape(2 * tok, heads_kv, HEAD_SIZE)
        .astype(jnp.bfloat16)
    )
    both = jnp.stack([key_rows, value_rows])
    paired, relayed = both[:, :tok], both[:, tok:]
    slots = [(paired, position), (relayed, jnp.where(g == 1, x, -1))]
    for d in sorted(range(1, width), key=lambda d: (-min(d, width - d), d)):
        send = jnp.where((g == 1) & (x + d >= width), relayed, paired)
        pairs = [(j, j + d) for j in range(width - d)]
        pairs += [(width + j, width + (j + d) % width) for j in range(width)]
        moved = exchange(send, "context", pairs)
        slots.append((moved, jnp.where(x >= d, position - d, jnp.where(g == 1, x - d + width, -1))))
    for e in range(1, reach - width + 1):
        moved = exchange(relayed, "context", [(width + j, width + j + e) for j in range(width - e)])
        slots.append((moved, jnp.where((g == 1) & (x >= e), x - e, -1)))
    keys_all = jnp.concatenate([blk[0] for blk, _ in slots], axis=0)
    values_all = jnp.concatenate([blk[1] for blk, _ in slots], axis=0)
    ids = doc_ids[0]
    key_pos = jnp.concatenate(
        [jnp.where(src >= 0, src * tok + jnp.arange(tok, dtype=jnp.int32), -1) for _, src in slots]
    )
    key_doc = jnp.concatenate(
        [lax.dynamic_slice_in_dim(ids, jnp.maximum(src, 0) * tok, tok, 0) for _, src in slots]
    )
    query_doc = lax.dynamic_slice_in_dim(ids, position * tok, tok, 0)
    allowed = (
        (key_pos[None, :] <= query_pos[:, None])
        & (key_pos[None, :] >= 0)
        & (key_doc[None, :] == query_doc[:, None])
    )
    grouped_queries = queries[0].reshape(tok, heads_kv, group, HEAD_SIZE)
    early = len(slots) - 3
    scores = jnp.concatenate(
        [
            jnp.einsum(
                "qhgd,khd->hgqk",
                grouped_queries,
                jnp.concatenate([blk[0] for blk, _ in part], axis=0),
                preferred_element_type=jnp.float32,
            )
            for part in (slots[:early], slots[early:])
        ],
        axis=-1,
    ) * scale
    scores = jnp.where(allowed[None, None], scores, NEG)
    maxima = jnp.max(scores, axis=-1)
    weights = jnp.where(allowed[None, None], jnp.exp(scores - maxima[..., None]), 0.0)
    totals = jnp.sum(weights, axis=-1)
    sums = jnp.einsum(
        "hgqk,khd->qhgd", weights.astype(jnp.bfloat16), values_all, preferred_element_type=jnp.float32
    )
    result = sums / jnp.transpose(totals, (2, 0, 1))[..., None]
    result = result.reshape(tok, heads_q * HEAD_SIZE).astype(jnp.bfloat16)
    return result[None]


def solution(mesh):
    return jax.shard_map(
        functools.partial(shards, mesh.shape["dp"], mesh.shape["context"]),
        mesh=mesh,
        in_specs=(P("dp", "context", None), P("dp", "context", None), P("dp", None), P("dp", None)),
        out_specs=P("dp", "context", None),
        check_vma=False,
    )
```

```python
import functools

import jax
import jax.numpy as jnp
from jax import lax
from jax.sharding import PartitionSpec as P

HEAD_SIZE = 128
DOC_MOST = 1152

NEG = -1e30


def apply_rotation(key_rows, positions):
    half = key_rows.shape[-1] // 2
    freq = 500000.0 ** (-(jnp.arange(half, dtype=jnp.float32) * 2.0 / key_rows.shape[-1]))
    angle = positions.astype(jnp.float32)[:, None] * freq[None, :]
    cosine = jnp.cos(angle)[:, None, :]
    sine = jnp.sin(angle)[:, None, :]
    first = key_rows[..., :half]
    second = key_rows[..., half:]
    return jnp.concatenate(
        [first * cosine - second * sine, second * cosine + first * sine], axis=-1
    )


def exchange(block, axis_name, pairs):
    return lax.ppermute(block, axis_name, pairs)


def gather_rows(block, n_dp, after_z):
    nc, ny = 2, 8
    nz = n_dp // (nc * ny)
    index = lax.axis_index("dp")
    z, y, core = index // (ny * nc), (index // nc) % ny, index % nc
    buf = block[None]
    for b in reversed(range(nz.bit_length() - 1)):
        m = (1 << b) * ny * nc
        other = exchange(buf, "dp", [(j, j ^ m) for j in range(n_dp)])
        low_side = ((z >> b) & 1) == 0
        lo = jnp.where(low_side, buf, other)
        hi = jnp.where(low_side, other, buf)
        buf = jnp.concatenate([lo[:, None], hi[:, None]], axis=1).reshape((-1,) + block.shape)

    buf, held = lax.optimization_barrier((buf, after_z[0]))
    sent = exchange(held, after_z[1], after_z[2])

    def along_y(step):
        return [(j, (j // (ny * nc)) * ny * nc + ((j // nc + step) % ny) * nc + j % nc) for j in range(n_dp)]

    forward, backward = buf, buf
    ahead, behind = [], []
    for t in range(1, ny // 2 + 1):
        forward = exchange(forward, "dp", along_y(1))
        behind.append(forward)
    for t in range(1, ny - ny // 2):
        backward = exchange(backward, "dp", along_y(-1))
        ahead.append(backward)
    pieces = jnp.stack([buf] + ahead + behind[::-1])
    pieces, sent = lax.optimization_barrier((pieces, sent))
    pieces = jnp.roll(pieces, y, axis=0)
    other = exchange(pieces, "dp", [(j, j ^ 1) for j in range(n_dp)])
    first = jnp.where(core == 0, pieces, other)
    second = jnp.where(core == 0, other, pieces)
    full = jnp.transpose(jnp.stack([first, second], axis=2), (1, 0, 2, 3, 4))
    return full.reshape((-1,) + block.shape[1:]), sent


def shards(n_dp, n_ctx, hidden_in, queries, kv_weight, doc_ids):
    acts = hidden_in[0]
    tok = acts.shape[0]
    columns = kv_weight.shape[1]
    heads_kv = columns // (2 * HEAD_SIZE)
    heads_q = queries.shape[2] // HEAD_SIZE
    group = heads_q // heads_kv
    scale = 1.0 / float(HEAD_SIZE) ** 0.5
    position = lax.axis_index("context")
    reach = min(n_ctx - 1, -(-(DOC_MOST - 1) // tok))
    width = n_ctx // 2
    g, x = position // width, position % width
    relay = (acts, "context", [(j, width + j) for j in range(width)])
    weight, relayed_acts = gather_rows(kv_weight, n_dp, relay)
    query_pos = position * tok + jnp.arange(tok, dtype=jnp.int32)
    both_pos = jnp.concatenate([query_pos, x * tok + jnp.arange(tok, dtype=jnp.int32)])
    key_value = jnp.dot(
        jnp.concatenate([acts, relayed_acts], axis=0), weight, preferred_element_type=jnp.float32
    )
    key_rows = apply_rotation(
        key_value[:, : heads_kv * HEAD_SIZE].reshape(2 * tok, heads_kv, HEAD_SIZE), both_pos
    ).astype(jnp.bfloat16)
    value_rows = (
        key_value[:, heads_kv * HEAD_SIZE :]
        .reshape(2 * tok, heads_kv, HEAD_SIZE)
        .astype(jnp.bfloat16)
    )
    both = jnp.stack([key_rows, value_rows])
    paired, relayed = both[:, :tok], both[:, tok:]
    slots = [(paired, position), (relayed, jnp.where(g == 1, x, -1))]
    for d in sorted(range(1, width), key=lambda d: (-min(d, width - d), d)):
        send = jnp.where((g == 1) & (x + d >= width), relayed, paired)
        pairs = [(j, j + d) for j in range(width - d)]
        pairs += [(width + j, width + (j + d) % width) for j in range(width)]
        moved = exchange(send, "context", pairs)
        slots.append((moved, jnp.where(x >= d, position - d, jnp.where(g == 1, x - d + width, -1))))
    for e in range(1, reach - width + 1):
        moved = exchange(relayed, "context", [(width + j, width + j + e) for j in range(width - e)])
        slots.append((moved, jnp.where((g == 1) & (x >= e), x - e, -1)))
    keys_all = jnp.concatenate([blk[0] for blk, _ in slots], axis=0)
    values_all = jnp.concatenate([blk[1] for blk, _ in slots], axis=0)
    ids = doc_ids[0]
    key_pos = jnp.concatenate(
        [jnp.where(src >= 0, src * tok + jnp.arange(tok, dtype=jnp.int32), -1) for _, src in slots]
    )
    key_doc = jnp.concatenate(
        [lax.dynamic_slice_in_dim(ids, jnp.maximum(src, 0) * tok, tok, 0) for _, src in slots]
    )
    query_doc = lax.dynamic_slice_in_dim(ids, position * tok, tok, 0)
    allowed = (
        (key_pos[None, :] <= query_pos[:, None])
        & (key_pos[None, :] >= 0)
        & (key_doc[None, :] == query_doc[:, None])
    )
    grouped_queries = queries[0].reshape(tok, heads_kv, group, HEAD_SIZE)
    early = len(slots) - 3
    cut = early * tok

    def chunk(part, mask, floor):
        scores = (
            jnp.einsum(
                "qhgd,khd->hgqk",
                grouped_queries,
                jnp.concatenate([blk[0] for blk, _ in part], axis=0),
                preferred_element_type=jnp.float32,
            )
            * scale
        )
        scores = jnp.where(mask[None, None], scores, NEG)
        maxima = jnp.maximum(floor, jnp.max(scores, axis=-1))
        weights = jnp.where(mask[None, None], jnp.exp(scores - maxima[..., None]), 0.0)
        sums = jnp.einsum(
            "hgqk,khd->qhgd",
            weights.astype(jnp.bfloat16),
            jnp.concatenate([blk[1] for blk, _ in part], axis=0),
            preferred_element_type=jnp.float32,
        )
        return maxima, jnp.sum(weights, axis=-1), sums

    first_max, first_total, first_sums = chunk(slots[:early], allowed[:, :cut], NEG)
    maxima, late_total, late_sums = chunk(slots[early:], allowed[:, cut:], first_max)
    kept = jnp.exp(first_max - maxima)
    totals = first_total * kept + late_total
    sums = first_sums * jnp.transpose(kept, (2, 0, 1))[..., None] + late_sums
    result = sums / jnp.transpose(totals, (2, 0, 1))[..., None]
    result = result.reshape(tok, heads_q * HEAD_SIZE).astype(jnp.bfloat16)
    return result[None]


def solution(mesh):
    return jax.shard_map(
        functools.partial(shards, mesh.shape["dp"], mesh.shape["context"]),
        mesh=mesh,
        in_specs=(P("dp", "context", None), P("dp", "context", None), P("dp", None), P("dp", None)),
        out_specs=P("dp", "context", None),
        check_vma=False,
    )
```

```python
import functools

import jax
import jax.numpy as jnp
from jax import lax
from jax.sharding import PartitionSpec as P

HEAD_SIZE = 128
DOC_MOST = 1152

NEG = -1e30


def apply_rotation(key_rows, positions):
    half = key_rows.shape[-1] // 2
    freq = 500000.0 ** (-(jnp.arange(half, dtype=jnp.float32) * 2.0 / key_rows.shape[-1]))
    angle = positions.astype(jnp.float32)[:, None] * freq[None, :]
    cosine = jnp.cos(angle)[:, None, :]
    sine = jnp.sin(angle)[:, None, :]
    first = key_rows[..., :half]
    second = key_rows[..., half:]
    return jnp.concatenate(
        [first * cosine - second * sine, second * cosine + first * sine], axis=-1
    )


def exchange(block, axis_name, pairs):
    return lax.ppermute(block, axis_name, pairs)


def gather_rows(block, n_dp, after_z):
    nc, ny = 2, 8
    nz = n_dp // (nc * ny)
    index = lax.axis_index("dp")
    z, y, core = index // (ny * nc), (index // nc) % ny, index % nc
    buf = block[None]
    for b in reversed(range(nz.bit_length() - 1)):
        m = (1 << b) * ny * nc
        other = exchange(buf, "dp", [(j, j ^ m) for j in range(n_dp)])
        low_side = ((z >> b) & 1) == 0
        lo = jnp.where(low_side, buf, other)
        hi = jnp.where(low_side, other, buf)
        buf = jnp.concatenate([lo[:, None], hi[:, None]], axis=1).reshape((-1,) + block.shape)

    buf, held = lax.optimization_barrier((buf, after_z[0]))
    sent = exchange(held, after_z[1], after_z[2])

    def along_y(step):
        return [(j, (j // (ny * nc)) * ny * nc + ((j // nc + step) % ny) * nc + j % nc) for j in range(n_dp)]

    forward, backward = buf, buf
    ahead, behind = [], []
    for t in range(1, ny // 2 + 1):
        forward = exchange(forward, "dp", along_y(1))
        behind.append(forward)
    for t in range(1, ny - ny // 2):
        backward = exchange(backward, "dp", along_y(-1))
        ahead.append(backward)
    pieces = jnp.stack([buf] + ahead + behind[::-1])
    pieces, sent = lax.optimization_barrier((pieces, sent))
    pieces = jnp.roll(pieces, y, axis=0)
    other = exchange(pieces, "dp", [(j, j ^ 1) for j in range(n_dp)])
    first = jnp.where(core == 0, pieces, other)
    second = jnp.where(core == 0, other, pieces)
    full = jnp.transpose(jnp.stack([first, second], axis=2), (1, 0, 2, 3, 4))
    return full.reshape((-1,) + block.shape[1:]), sent


def shards(n_dp, n_ctx, hidden_in, queries, kv_weight, doc_ids):
    acts = hidden_in[0]
    tok = acts.shape[0]
    columns = kv_weight.shape[1]
    heads_kv = columns // (2 * HEAD_SIZE)
    heads_q = queries.shape[2] // HEAD_SIZE
    group = heads_q // heads_kv
    scale = 1.0 / float(HEAD_SIZE) ** 0.5
    position = lax.axis_index("context")
    reach = min(n_ctx - 1, -(-(DOC_MOST - 1) // tok))
    width = n_ctx // 2
    g, x = position // width, position % width
    relay = (acts, "context", [(j, width + j) for j in range(width)])
    weight, relayed_acts = gather_rows(kv_weight, n_dp, relay)
    query_pos = position * tok + jnp.arange(tok, dtype=jnp.int32)
    both_pos = jnp.concatenate([query_pos, x * tok + jnp.arange(tok, dtype=jnp.int32)])
    key_value = jnp.dot(
        jnp.concatenate([acts, relayed_acts], axis=0), weight, preferred_element_type=jnp.float32
    )
    key_rows = apply_rotation(
        key_value[:, : heads_kv * HEAD_SIZE].reshape(2 * tok, heads_kv, HEAD_SIZE), both_pos
    ).astype(jnp.bfloat16)
    value_rows = (
        key_value[:, heads_kv * HEAD_SIZE :]
        .reshape(2 * tok, heads_kv, HEAD_SIZE)
        .astype(jnp.bfloat16)
    )
    both = jnp.stack([key_rows, value_rows])
    paired, relayed = both[:, :tok], both[:, tok:]
    slots = [(paired, position), (relayed, jnp.where(g == 1, x, -1))]
    for e in range(1, reach - width + 1):
        moved = exchange(relayed, "context", [(width + j, width + j + e) for j in range(width - e)])
        slots.append((moved, jnp.where((g == 1) & (x >= e), x - e, -1)))
    for d in sorted(range(1, width), key=lambda d: (-min(d, width - d), d)):
        send = jnp.where((g == 1) & (x + d >= width), relayed, paired)
        pairs = [(j, j + d) for j in range(width - d)]
        pairs += [(width + j, width + (j + d) % width) for j in range(width)]
        moved = exchange(send, "context", pairs)
        slots.append((moved, jnp.where(x >= d, position - d, jnp.where(g == 1, x - d + width, -1))))
    keys_all = jnp.concatenate([blk[0] for blk, _ in slots], axis=0)
    values_all = jnp.concatenate([blk[1] for blk, _ in slots], axis=0)
    ids = doc_ids[0]
    key_pos = jnp.concatenate(
        [jnp.where(src >= 0, src * tok + jnp.arange(tok, dtype=jnp.int32), -1) for _, src in slots]
    )
    key_doc = jnp.concatenate(
        [lax.dynamic_slice_in_dim(ids, jnp.maximum(src, 0) * tok, tok, 0) for _, src in slots]
    )
    query_doc = lax.dynamic_slice_in_dim(ids, position * tok, tok, 0)
    allowed = (
        (key_pos[None, :] <= query_pos[:, None])
        & (key_pos[None, :] >= 0)
        & (key_doc[None, :] == query_doc[:, None])
    )
    grouped_queries = queries[0].reshape(tok, heads_kv, group, HEAD_SIZE)
    early = len(slots) - 3
    scores = jnp.concatenate(
        [
            jnp.einsum(
                "qhgd,khd->hgqk",
                grouped_queries,
                jnp.concatenate([blk[0] for blk, _ in part], axis=0),
                preferred_element_type=jnp.float32,
            )
            for part in (slots[:early], slots[early:])
        ],
        axis=-1,
    ) * scale
    scores = jnp.where(allowed[None, None], scores, NEG)
    maxima = jnp.max(scores, axis=-1)
    weights = jnp.where(allowed[None, None], jnp.exp(scores - maxima[..., None]), 0.0)
    totals = jnp.sum(weights, axis=-1)
    sums = jnp.einsum(
        "hgqk,khd->qhgd", weights.astype(jnp.bfloat16), values_all, preferred_element_type=jnp.float32
    )
    result = sums / jnp.transpose(totals, (2, 0, 1))[..., None]
    result = result.reshape(tok, heads_q * HEAD_SIZE).astype(jnp.bfloat16)
    return result[None]


def solution(mesh):
    return jax.shard_map(
        functools.partial(shards, mesh.shape["dp"], mesh.shape["context"]),
        mesh=mesh,
        in_specs=(P("dp", "context", None), P("dp", "context", None), P("dp", None), P("dp", None)),
        out_specs=P("dp", "context", None),
        check_vma=False,
    )
```

```python
import functools

import jax
import jax.numpy as jnp
from jax import lax
from jax.sharding import PartitionSpec as P

HEAD_SIZE = 128
DOC_MOST = 1152

NEG = -1e30


def apply_rotation(key_rows, positions):
    half = key_rows.shape[-1] // 2
    freq = 500000.0 ** (-(jnp.arange(half, dtype=jnp.float32) * 2.0 / key_rows.shape[-1]))
    angle = positions.astype(jnp.float32)[:, None] * freq[None, :]
    cosine = jnp.cos(angle)[:, None, :]
    sine = jnp.sin(angle)[:, None, :]
    first = key_rows[..., :half]
    second = key_rows[..., half:]
    return jnp.concatenate(
        [first * cosine - second * sine, second * cosine + first * sine], axis=-1
    )


def exchange(block, axis_name, pairs):
    return lax.ppermute(block, axis_name, pairs)


def gather_rows(block, n_dp, after_z):
    nc, ny = 2, 8
    nz = n_dp // (nc * ny)
    index = lax.axis_index("dp")
    z, y, core = index // (ny * nc), (index // nc) % ny, index % nc
    buf = block[None]
    for b in reversed(range(nz.bit_length() - 1)):
        m = (1 << b) * ny * nc
        other = exchange(buf, "dp", [(j, j ^ m) for j in range(n_dp)])
        low_side = ((z >> b) & 1) == 0
        lo = jnp.where(low_side, buf, other)
        hi = jnp.where(low_side, other, buf)
        buf = jnp.concatenate([lo[:, None], hi[:, None]], axis=1).reshape((-1,) + block.shape)

    buf, held = lax.optimization_barrier((buf, after_z[0]))
    sent = exchange(held, after_z[1], after_z[2])

    def along_y(step):
        return [(j, (j // (ny * nc)) * ny * nc + ((j // nc + step) % ny) * nc + j % nc) for j in range(n_dp)]

    forward, backward = buf, buf
    ahead, behind = [], []
    for t in range(1, ny // 2 + 1):
        forward = exchange(forward, "dp", along_y(1))
        behind.append(forward)
    for t in range(1, ny - ny // 2):
        backward = exchange(backward, "dp", along_y(-1))
        ahead.append(backward)
    pieces = jnp.stack([buf] + ahead + behind[::-1])
    pieces, sent = lax.optimization_barrier((pieces, sent))
    pieces = jnp.roll(pieces, y, axis=0)
    other = exchange(pieces, "dp", [(j, j ^ 1) for j in range(n_dp)])
    first = jnp.where(core == 0, pieces, other)
    second = jnp.where(core == 0, other, pieces)
    full = jnp.transpose(jnp.stack([first, second], axis=2), (1, 0, 2, 3, 4))
    return full.reshape((-1,) + block.shape[1:]), sent


def shards(n_dp, n_ctx, hidden_in, queries, kv_weight, doc_ids):
    acts = hidden_in[0]
    tok = acts.shape[0]
    columns = kv_weight.shape[1]
    heads_kv = columns // (2 * HEAD_SIZE)
    heads_q = queries.shape[2] // HEAD_SIZE
    group = heads_q // heads_kv
    scale = 1.0 / float(HEAD_SIZE) ** 0.5
    position = lax.axis_index("context")
    reach = min(n_ctx - 1, -(-(DOC_MOST - 1) // tok))
    width = n_ctx // 2
    g, x = position // width, position % width
    relay = (acts, "context", [(j, width + j) for j in range(width)])
    weight, relayed_acts = gather_rows(kv_weight, n_dp, relay)
    query_pos = position * tok + jnp.arange(tok, dtype=jnp.int32)
    both_pos = jnp.concatenate([query_pos, x * tok + jnp.arange(tok, dtype=jnp.int32)])
    key_value = jnp.dot(
        jnp.concatenate([acts, relayed_acts], axis=0), weight, preferred_element_type=jnp.float32
    )
    key_rows = apply_rotation(
        key_value[:, : heads_kv * HEAD_SIZE].reshape(2 * tok, heads_kv, HEAD_SIZE), both_pos
    ).astype(jnp.bfloat16)
    value_rows = (
        key_value[:, heads_kv * HEAD_SIZE :]
        .reshape(2 * tok, heads_kv, HEAD_SIZE)
        .astype(jnp.bfloat16)
    )
    both = jnp.stack([key_rows, value_rows])
    paired, relayed = both[:, :tok], both[:, tok:]
    slots = [(paired, position), (relayed, jnp.where(g == 1, x, -1))]
    for d in sorted(range(1, width), key=lambda d: (-min(d, width - d), d)):
        send = jnp.where((g == 1) & (x + d >= width), relayed, paired)
        pairs = [(j, j + d) for j in range(width - d)]
        pairs += [(width + j, width + (j + d) % width) for j in range(width)]
        moved = exchange(send, "context", pairs)
        slots.append((moved, jnp.where(x >= d, position - d, jnp.where(g == 1, x - d + width, -1))))
    for e in range(1, reach - width + 1):
        moved = exchange(relayed, "context", [(width + j, width + j + e) for j in range(width - e)])
        slots.append((moved, jnp.where((g == 1) & (x >= e), x - e, -1)))
    keys_all = jnp.concatenate([blk[0] for blk, _ in slots], axis=0)
    values_all = jnp.concatenate([blk[1] for blk, _ in slots], axis=0)
    ids = doc_ids[0]
    key_pos = jnp.concatenate(
        [jnp.where(src >= 0, src * tok + jnp.arange(tok, dtype=jnp.int32), -1) for _, src in slots]
    )
    key_doc = jnp.concatenate(
        [lax.dynamic_slice_in_dim(ids, jnp.maximum(src, 0) * tok, tok, 0) for _, src in slots]
    )
    query_doc = lax.dynamic_slice_in_dim(ids, position * tok, tok, 0)
    allowed = (
        (key_pos[None, :] <= query_pos[:, None])
        & (key_pos[None, :] >= 0)
        & (key_doc[None, :] == query_doc[:, None])
    )
    grouped_queries = queries[0].reshape(tok, heads_kv, group, HEAD_SIZE)
    cuts = [0, len(slots) - 5, len(slots) - 3, len(slots)]
    scores = jnp.concatenate(
        [
            jnp.einsum(
                "qhgd,khd->hgqk",
                grouped_queries,
                jnp.concatenate([blk[0] for blk, _ in part], axis=0),
                preferred_element_type=jnp.float32,
            )
            for part in (slots[a:b] for a, b in zip(cuts[:-1], cuts[1:]))
        ],
        axis=-1,
    ) * scale
    scores = jnp.where(allowed[None, None], scores, NEG)
    maxima = jnp.max(scores, axis=-1)
    weights = jnp.where(allowed[None, None], jnp.exp(scores - maxima[..., None]), 0.0)
    totals = jnp.sum(weights, axis=-1)
    sums = jnp.einsum(
        "hgqk,khd->qhgd", weights.astype(jnp.bfloat16), values_all, preferred_element_type=jnp.float32
    )
    result = sums / jnp.transpose(totals, (2, 0, 1))[..., None]
    result = result.reshape(tok, heads_q * HEAD_SIZE).astype(jnp.bfloat16)
    return result[None]


def solution(mesh):
    return jax.shard_map(
        functools.partial(shards, mesh.shape["dp"], mesh.shape["context"]),
        mesh=mesh,
        in_specs=(P("dp", "context", None), P("dp", "context", None), P("dp", None), P("dp", None)),
        out_specs=P("dp", "context", None),
        check_vma=False,
    )
```

```python
import functools

import jax
import jax.numpy as jnp
from jax import lax
from jax.sharding import PartitionSpec as P

HEAD_SIZE = 128
DOC_MOST = 1152

NEG = -1e30


def apply_rotation(key_rows, positions):
    half = key_rows.shape[-1] // 2
    freq = 500000.0 ** (-(jnp.arange(half, dtype=jnp.float32) * 2.0 / key_rows.shape[-1]))
    angle = positions.astype(jnp.float32)[:, None] * freq[None, :]
    cosine = jnp.cos(angle)[:, None, :]
    sine = jnp.sin(angle)[:, None, :]
    first = key_rows[..., :half]
    second = key_rows[..., half:]
    return jnp.concatenate(
        [first * cosine - second * sine, second * cosine + first * sine], axis=-1
    )


def exchange(block, axis_name, pairs):
    return lax.ppermute(block, axis_name, pairs)


def gather_rows(block, n_dp, after_z):
    nc, ny = 2, 8
    nz = n_dp // (nc * ny)
    index = lax.axis_index("dp")
    z, y, core = index // (ny * nc), (index // nc) % ny, index % nc
    buf = block[None]
    for b in reversed(range(nz.bit_length() - 1)):
        m = (1 << b) * ny * nc
        other = exchange(buf, "dp", [(j, j ^ m) for j in range(n_dp)])
        low_side = ((z >> b) & 1) == 0
        lo = jnp.where(low_side, buf, other)
        hi = jnp.where(low_side, other, buf)
        buf = jnp.concatenate([lo[:, None], hi[:, None]], axis=1).reshape((-1,) + block.shape)

    buf, held = lax.optimization_barrier((buf, after_z[0]))
    sent = exchange(held, after_z[1], after_z[2])

    def along_y(step):
        return [(j, (j // (ny * nc)) * ny * nc + ((j // nc + step) % ny) * nc + j % nc) for j in range(n_dp)]

    forward, backward = buf, buf
    ahead, behind = [], []
    for t in range(1, ny // 2 + 1):
        forward = exchange(forward, "dp", along_y(1))
        behind.append(forward)
    for t in range(1, ny - ny // 2):
        backward = exchange(backward, "dp", along_y(-1))
        ahead.append(backward)
    pieces = jnp.stack([buf] + ahead + behind[::-1])
    pieces, sent = lax.optimization_barrier((pieces, sent))
    pieces = jnp.roll(pieces, y, axis=0)
    other = exchange(pieces, "dp", [(j, j ^ 1) for j in range(n_dp)])
    first = jnp.where(core == 0, pieces, other)
    second = jnp.where(core == 0, other, pieces)
    full = jnp.transpose(jnp.stack([first, second], axis=2), (1, 0, 2, 3, 4))
    return full.reshape((-1,) + block.shape[1:]), sent


def shards(n_dp, n_ctx, hidden_in, queries, kv_weight, doc_ids):
    acts = hidden_in[0]
    tok = acts.shape[0]
    columns = kv_weight.shape[1]
    heads_kv = columns // (2 * HEAD_SIZE)
    heads_q = queries.shape[2] // HEAD_SIZE
    group = heads_q // heads_kv
    scale = 1.0 / float(HEAD_SIZE) ** 0.5
    position = lax.axis_index("context")
    reach = min(n_ctx - 1, -(-(DOC_MOST - 1) // tok))
    width = n_ctx // 2
    g, x = position // width, position % width
    relay = (acts, "context", [(j, width + j) for j in range(width)])
    weight, relayed_acts = gather_rows(kv_weight, n_dp, relay)
    query_pos = position * tok + jnp.arange(tok, dtype=jnp.int32)
    both_pos = jnp.concatenate([query_pos, x * tok + jnp.arange(tok, dtype=jnp.int32)])
    key_value = jnp.dot(
        jnp.concatenate([acts, relayed_acts], axis=0), weight, preferred_element_type=jnp.float32
    )
    key_rows = apply_rotation(
        key_value[:, : heads_kv * HEAD_SIZE].reshape(2 * tok, heads_kv, HEAD_SIZE), both_pos
    ).astype(jnp.bfloat16)
    value_rows = (
        key_value[:, heads_kv * HEAD_SIZE :]
        .reshape(2 * tok, heads_kv, HEAD_SIZE)
        .astype(jnp.bfloat16)
    )
    both = jnp.stack([key_rows, value_rows])
    paired, relayed = both[:, :tok], both[:, tok:]
    slots = [(paired, position), (relayed, jnp.where(g == 1, x, -1))]
    for d in sorted(range(1, width), key=lambda d: (-min(d, width - d), d)):
        send = jnp.where((g == 1) & (x + d >= width), relayed, paired)
        pairs = [(j, j + d) for j in range(width - d)]
        pairs += [(width + j, width + (j + d) % width) for j in range(width)]
        moved = exchange(send, "context", pairs)
        slots.append((moved, jnp.where(x >= d, position - d, jnp.where(g == 1, x - d + width, -1))))
    for e in range(1, reach - width + 1):
        moved = exchange(relayed, "context", [(width + j, width + j + e) for j in range(width - e)])
        slots.append((moved, jnp.where((g == 1) & (x >= e), x - e, -1)))
    keys_all = jnp.concatenate([blk[0] for blk, _ in slots], axis=0)
    values_all = jnp.concatenate([blk[1] for blk, _ in slots], axis=0)
    ids = doc_ids[0]
    key_pos = jnp.concatenate(
        [jnp.where(src >= 0, src * tok + jnp.arange(tok, dtype=jnp.int32), -1) for _, src in slots]
    )
    key_doc = jnp.concatenate(
        [lax.dynamic_slice_in_dim(ids, jnp.maximum(src, 0) * tok, tok, 0) for _, src in slots]
    )
    query_doc = lax.dynamic_slice_in_dim(ids, position * tok, tok, 0)
    allowed = (
        (key_pos[None, :] <= query_pos[:, None])
        & (key_pos[None, :] >= 0)
        & (key_doc[None, :] == query_doc[:, None])
    )
    grouped_queries = queries[0].reshape(tok, heads_kv, group, HEAD_SIZE)
    early = len(slots) - 2
    scores = jnp.concatenate(
        [
            jnp.einsum(
                "qhgd,khd->hgqk",
                grouped_queries,
                jnp.concatenate([blk[0] for blk, _ in part], axis=0),
                preferred_element_type=jnp.float32,
            )
            for part in (slots[:early], slots[early:])
        ],
        axis=-1,
    ) * scale
    scores = jnp.where(allowed[None, None], scores, NEG)
    maxima = jnp.max(scores, axis=-1)
    weights = jnp.where(allowed[None, None], jnp.exp(scores - maxima[..., None]), 0.0)
    totals = jnp.sum(weights, axis=-1)
    sums = jnp.einsum(
        "hgqk,khd->qhgd", weights.astype(jnp.bfloat16), values_all, preferred_element_type=jnp.float32
    )
    result = sums / jnp.transpose(totals, (2, 0, 1))[..., None]
    result = result.reshape(tok, heads_q * HEAD_SIZE).astype(jnp.bfloat16)
    return result[None]


def solution(mesh):
    return jax.shard_map(
        functools.partial(shards, mesh.shape["dp"], mesh.shape["context"]),
        mesh=mesh,
        in_specs=(P("dp", "context", None), P("dp", "context", None), P("dp", None), P("dp", None)),
        out_specs=P("dp", "context", None),
        check_vma=False,
    )
```
